512 devices in a mesh: grp: 16 (over z), wrk: 32 (over y, x, core).
Axes of the slice: x: 4, y: 4, z: 16, core: 2. Of those that a mesh axis runs over, the one named last changes fastest.
Arguments:
- orbitals: bfloat16 [512, 32, 1024], P(('grp', 'wrk')), may hold values from -6 to 6
- offsets: int32 [512, 3], replicated, may hold values from 0 to 135, as said below
- pair_slots: int32 [16, 32, 6, 2], P('grp', 'wrk'), may hold values from 0 to 511, as said below
- pair_count: int32 [16, 32], P('grp', 'wrk'), may hold values from 0 to 6, as said below
Outputs:
- exchange_fields: float32 [512, 32, 1024], P(('grp', 'wrk'))
The draws below stay inside these ranges and needn't reach their ends.
Inputs may be any that keep to these rules, and one draw needn't show every extreme that they name: Row o gives the grid point of the first cell of orbital o's box; offsets of orbitals of the same or adjacent groups differ by less than 32 in each coordinate. Every slot of pair_slots[g, w] holds an orbital a of group g (numbers g * 32 to g * 32 + 31) and an orbital b other than a of group g or g + 1, with offsets of a and b differing by less than 32 in each coordinate; slots at or past pair_count[g, w] hold entries of the same kind that are not pairs. `pair_count`: the counts of every group sum to 96; in every group one worker has 6 pairs and one has none.
All inputs are finite; a program needn't handle non-finite values.
Results may differ from the reference program's by a relative error of at most 0.0003.
Values may be sent and summed in bfloat16 or wider, within the bound.
No kernel may reach another device: no remote copies, remote signals or barrier semaphores. Data moves between devices by JAX's collectives and lax.ppermute only.
A program may use at most 64 MiB of HBM per device.

```python
import jax
import jax.numpy as jnp
from jax import lax

BOX = 32
ORB_DEV = 1
PAIR_DEV = 3
CAP = 6
GRP_ORBS = 32
ORBS = 512


def draw_orbitals(key, part):
    noise = jax.random.normal(jax.random.fold_in(key, 3), (ORBS, BOX, BOX * BOX), jnp.float32)
    cell_centres = (jnp.arange(BOX, dtype=jnp.float32) + 0.5) / BOX
    bump_line = jnp.sin(jnp.pi * cell_centres)
    envelope = 0.5 + bump_line[:, None, None] * bump_line[None, :, None] * bump_line[None, None, :]
    envelope = envelope.reshape(BOX, BOX * BOX)
    values = envelope * noise
    return jnp.clip(values, -6.0, 6.0).astype(jnp.bfloat16)


def draw_offsets(key, part):
    inner = jax.random.randint(jax.random.fold_in(key, 5), (ORBS, 3), 0, BOX // 2).astype(jnp.int32)
    inner = inner.at[0].set(jnp.zeros((3,), jnp.int32))
    inner = inner.at[ORBS - 1, 2].set(BOX // 2 - 1)
    layer_height = jnp.arange(ORBS, dtype=jnp.int32) // GRP_ORBS * (BOX // 4)
    lifting = jnp.stack([jnp.zeros_like(layer_height), jnp.zeros_like(layer_height), layer_height], axis=1)
    return (inner + lifting).astype(jnp.int32)


def pair_tables(key):
    base_key = jax.random.fold_in(key, 9)
    group_total = ORBS // GRP_ORBS
    worker_total = GRP_ORBS // ORB_DEV
    order_keys = jax.random.split(jax.random.fold_in(base_key, 1), group_total)
    orderings = jax.vmap(lambda single: jax.random.permutation(single, worker_total))(order_keys).astype(jnp.int32)
    half_count = worker_total // 2
    spread = jax.random.randint(jax.random.fold_in(base_key, 2), (group_total, half_count), 0, PAIR_DEV + 1).astype(jnp.int32)
    spread = spread.at[:, 0].set(PAIR_DEV)
    by_rank = jnp.concatenate([PAIR_DEV + spread, PAIR_DEV - spread], axis=1)
    group_rows = jnp.arange(group_total, dtype=jnp.int32)[:, None] * jnp.ones((1, worker_total), jnp.int32)
    counts = jnp.zeros((group_total, worker_total), jnp.int32).at[group_rows, orderings].set(by_rank)
    left_local = jax.random.randint(jax.random.fold_in(base_key, 3), (group_total, worker_total, CAP), 0, GRP_ORBS).astype(jnp.int32)
    group_ids = jnp.arange(group_total, dtype=jnp.int32)[:, None, None]
    reach_span = jnp.where(group_ids < group_total - 1, 2 * GRP_ORBS, GRP_ORBS)
    raw_steps = jax.random.randint(jax.random.fold_in(base_key, 4), (group_total, worker_total, CAP), 0, 1 << 20).astype(jnp.int32)
    stride = 1 + raw_steps % (reach_span - 1)
    right_local = (left_local + stride) % reach_span
    slot_pairs = jnp.stack([group_ids * GRP_ORBS + left_local, group_ids * GRP_ORBS + right_local], axis=-1)
    return (slot_pairs.astype(jnp.int32), counts.astype(jnp.int32))


def draw_pair_slots(key, part):
    return pair_tables(key)[0]


def draw_pair_count(key, part):
    return pair_tables(key)[1]


def setup_inputs(seed: int = 0) -> dict:
    streams_of = jax.random.split(jax.random.key(seed), 5)
    return {
        "orbitals": draw_orbitals(jax.random.fold_in(streams_of[4], 71), 0),
        "offsets": draw_offsets(jax.random.fold_in(streams_of[4], 71), 0),
        "pair_slots": draw_pair_slots(jax.random.fold_in(streams_of[4], 71), 0),
        "pair_count": draw_pair_count(jax.random.fold_in(streams_of[4], 71), 0),
    }


screen_shift = 0.05
highest = lax.Precision.HIGHEST

def sine_table(box_edge):
    counting = jnp.arange(box_edge, dtype=jnp.float32) + 1.0
    scaling = jnp.sqrt(2.0 / (box_edge + 1.0))
    return scaling * jnp.sin(jnp.pi * counting[:, None] * counting[None, :] / (box_edge + 1.0))

def inverse_symbol(box_edge):
    counting = jnp.arange(box_edge, dtype=jnp.float32) + 1.0
    eigen_one = 4.0 * jnp.sin(jnp.pi * counting / (2.0 * (box_edge + 1.0))) ** 2
    eigen_sum = eigen_one[:, None, None] + eigen_one[None, :, None] + eigen_one[None, None, :]
    return 1.0 / (eigen_sum + screen_shift)

def apply_sines(field_cube, sine_rows):
    spectrum = jnp.einsum('ka,abc->kbc', sine_rows, field_cube, precision=highest)
    spectrum = jnp.einsum('lb,kbc->klc', sine_rows, spectrum, precision=highest)
    return jnp.einsum('mc,klc->klm', sine_rows, spectrum, precision=highest)

def place_box(field_cube, offset_diff, box_edge):
    padded = jnp.pad(field_cube, box_edge)
    corner_at = (box_edge - offset_diff).astype(jnp.int32)
    return lax.dynamic_slice(padded, (corner_at[0], corner_at[1], corner_at[2]), (box_edge, box_edge, box_edge))

def reference(orbitals, offsets, pair_slots, pair_count):
    box_edge = BOX
    orbital_cubes = orbitals.reshape(ORBS, box_edge, box_edge, box_edge)
    sine_rows = sine_table(box_edge)
    symbol = inverse_symbol(box_edge)
    slot_cap = pair_slots.shape[2]
    listed = pair_slots.reshape(-1, 2)
    in_use = (jnp.arange(slot_cap, dtype=jnp.int32)[None, None, :] < pair_count[:, :, None]).reshape(-1).astype(jnp.float32)

    def one_pair(fields, packed):
        orbital_pair, weight = packed
        left_orb = orbital_pair[0]
        right_orb = orbital_pair[1]
        offset_diff = (offsets[right_orb] - offsets[left_orb]).astype(jnp.int32)
        left_cube = lax.dynamic_index_in_dim(orbital_cubes, left_orb, 0, keepdims=False).astype(jnp.float32)
        right_cube = lax.dynamic_index_in_dim(orbital_cubes, right_orb, 0, keepdims=False).astype(jnp.float32)
        moved_right = place_box(right_cube, offset_diff, box_edge)
        potential = apply_sines(apply_sines(left_cube * moved_right, sine_rows) * symbol, sine_rows)
        weighted = potential * weight
        to_left = weighted * moved_right
        to_right = place_box(weighted * left_cube, -offset_diff, box_edge)
        current = lax.dynamic_index_in_dim(fields, left_orb, 0, keepdims=False)
        fields = lax.dynamic_update_index_in_dim(fields, current + to_left, left_orb, 0)
        current = lax.dynamic_index_in_dim(fields, right_orb, 0, keepdims=False)
        fields = lax.dynamic_update_index_in_dim(fields, current + to_right, right_orb, 0)
        return (fields, None)
    start_fields = jnp.zeros((ORBS, box_edge, box_edge, box_edge), jnp.float32)
    fields, ignored = lax.scan(one_pair, start_fields, (listed, in_use))
    return fields.reshape(ORBS, box_edge, box_edge * box_edge)
```

```python
import jax
import jax.numpy as jnp
from jax import lax
from jax.sharding import PartitionSpec as P

screen_shift = 0.05
highest = lax.Precision.HIGHEST


def passed_along(value, axis, steps):
    count = lax.axis_size(axis)
    initial, last = (max(0, -steps), min(count, count - steps))
    return lax.ppermute(value, axis, [(source, source + steps) for source in range(initial, last)])


def sine_table(box_edge):
    counting = jnp.arange(box_edge, dtype=jnp.float32) + 1.0
    scaling = jnp.sqrt(2.0 / (box_edge + 1.0))
    return scaling * jnp.sin(jnp.pi * counting[:, None] * counting[None, :] / (box_edge + 1.0))


def inverse_symbol(box_edge):
    counting = jnp.arange(box_edge, dtype=jnp.float32) + 1.0
    eigen_one = 4.0 * jnp.sin(jnp.pi * counting / (2.0 * (box_edge + 1.0))) ** 2
    eigen_sum = eigen_one[:, None, None] + eigen_one[None, :, None] + eigen_one[None, None, :]
    return 1.0 / (eigen_sum + screen_shift)


def shift_matrices(offset_diff, box_edge):
    cell = jnp.arange(box_edge, dtype=jnp.int32)

    def one_axis(shift):
        return cell[None, None, :] == (cell[None, :, None] - shift[:, None, None])

    row_shift = one_axis(offset_diff[:, 0])
    along_y = one_axis(offset_diff[:, 1])
    along_z = one_axis(offset_diff[:, 2])
    count = offset_diff.shape[0]
    plane_shift = (along_y[:, :, None, :, None] & along_z[:, None, :, None, :]).reshape(
        count, box_edge * box_edge, box_edge * box_edge
    )
    return row_shift.astype(jnp.float32), plane_shift.astype(jnp.bfloat16)


def move_bf16(boxes, row_shift, plane_shift):
    planes = jnp.einsum("pxc,pyc->pxy", boxes, plane_shift, preferred_element_type=jnp.float32)
    return jnp.einsum("pxa,pac->pxc", row_shift, planes, precision=highest)


def unmove_f32(fields, row_shift, plane_shift):
    rows = jnp.einsum("pax,pac->pxc", row_shift, fields, precision=highest)
    high = lax.reduce_precision(rows, exponent_bits=8, mantissa_bits=7)
    rest = rows - high
    middle = lax.reduce_precision(rest, exponent_bits=8, mantissa_bits=7)
    low = rest - middle
    parts = jnp.concatenate([high, middle, low], axis=1).astype(jnp.bfloat16)
    moved = jnp.einsum("pxc,pcy->pxy", parts, plane_shift, preferred_element_type=jnp.float32)
    box_edge = fields.shape[1]
    return (moved[:, :box_edge] + moved[:, box_edge : 2 * box_edge]) + moved[:, 2 * box_edge :]


def solve_boxes(density, sine_rows, plane_sines, symbol):
    count_boxes, box_edge, plane_size = density.shape

    def apply_sines(field_block):
        along_first = jnp.einsum("kx,nxf->nkf", sine_rows, field_block, precision=highest)
        flat_rows = along_first.reshape(count_boxes * box_edge, plane_size)
        along_plane = jnp.dot(
            flat_rows, plane_sines, precision=highest, preferred_element_type=jnp.float32
        )
        return along_plane.reshape(count_boxes, box_edge, plane_size)

    spectrum = apply_sines(density) * symbol
    return apply_sines(spectrum)


def corner_of(orbital, offsets):
    listing = jnp.arange(offsets.shape[0], dtype=jnp.int32)
    chosen = orbital[:, None] == listing[None, :]
    return jnp.sum(jnp.where(chosen[:, :, None], offsets[None, :, :], 0), axis=1, dtype=jnp.int32)


def rows_to_orbitals(fields, rows, count):
    chosen = rows[:, None] == jnp.arange(count, dtype=jnp.int32)[None, :]
    return jnp.sum(
        jnp.where(chosen[:, :, None, None], fields[:, None, :, :], 0.0), axis=0
    )


def local(orbitals, offsets, pair_slots, pair_count):
    orb_dev, box_edge, plane_size = orbitals.shape
    workers = lax.axis_size("wrk")
    group_index = lax.axis_index("grp")
    worker_index = lax.axis_index("wrk")
    grp_orbs = orb_dev * workers
    upper_set = passed_along(orbitals, "grp", -1)
    local_set = jnp.stack([orbitals, upper_set], axis=0)
    group_set = lax.all_gather(local_set, "wrk", axis=1, tiled=True)
    group_set = group_set.reshape(2 * grp_orbs, box_edge, plane_size)

    slot_cap = pair_slots.shape[2]
    per_worker = (slot_cap + 1) // 2
    group_slots = lax.all_gather(pair_slots[0, 0], "wrk").reshape(-1, 2)
    group_count = lax.all_gather(pair_count[0], "wrk").reshape(-1)
    in_use = (jnp.arange(slot_cap, dtype=jnp.int32)[None, :] < group_count[:, None]).reshape(-1)
    rank = jnp.cumsum(in_use.astype(jnp.int32)) - 1
    wanted = worker_index * per_worker + jnp.arange(per_worker, dtype=jnp.int32)
    match = in_use[None, :] & (rank[None, :] == wanted[:, None])
    pair_list = jnp.sum(jnp.where(match[:, :, None], group_slots[None, :, :], 0), axis=1)
    weights = jnp.any(match, axis=1).astype(jnp.float32)

    base = group_index * grp_orbs
    left_orb = jnp.where(weights > 0, pair_list[:, 0], base)
    right_orb = jnp.where(weights > 0, pair_list[:, 1], base)
    offset_diff = corner_of(right_orb, offsets) - corner_of(left_orb, offsets)
    left_row = jnp.clip(left_orb - base, 0, 2 * grp_orbs - 1)
    right_row = jnp.clip(right_orb - base, 0, 2 * grp_orbs - 1)
    left_boxes = jnp.take(group_set, left_row, axis=0)
    right_boxes = jnp.take(group_set, right_row, axis=0)
    row_shift, plane_shift = shift_matrices(offset_diff, box_edge)
    right_field = move_bf16(right_boxes, row_shift, plane_shift)

    sine_rows = sine_table(box_edge)
    plane_sines = (sine_rows[:, None, :, None] * sine_rows[None, :, None, :]).reshape(
        plane_size, plane_size
    )
    symbol = inverse_symbol(box_edge).reshape(box_edge, plane_size)
    left_field = left_boxes.astype(jnp.float32)
    potential = solve_boxes(left_field * right_field, sine_rows, plane_sines, symbol)
    weighted = potential * weights[:, None, None]
    to_left = weighted * right_field
    to_right = unmove_f32(weighted * left_field, row_shift, plane_shift)

    upper = right_row >= grp_orbs
    sent_fields = jnp.where(upper[:, None, None], to_right, 0.0)
    sent_rows = jnp.where(upper, right_row - grp_orbs, 0)
    got_fields = passed_along(sent_fields, "grp", 1)
    got_rows = passed_along(sent_rows, "grp", 1)

    kept_right = jnp.where(upper[:, None, None], 0.0, to_right)
    kept_rows = jnp.where(upper, 0, right_row)
    fields = jnp.concatenate([to_left, kept_right, got_fields], axis=0)
    rows = jnp.concatenate([left_row, kept_rows, got_rows], axis=0)
    combined = rows_to_orbitals(fields, rows, grp_orbs)
    return lax.psum_scatter(combined, "wrk", scatter_dimension=0, tiled=True)


def solution(mesh):
    return jax.shard_map(
        local,
        mesh=mesh,
        in_specs=(P(("grp", "wrk"), None, None), P(), P("grp", "wrk", None, None), P("grp", "wrk")),
        out_specs=P(("grp", "wrk"), None, None),
        check_vma=False,
    )
```

```python
import jax
import jax.numpy as jnp
from jax import lax
from jax.sharding import PartitionSpec as P

screen_shift = 0.05
highest = lax.Precision.HIGHEST
EXCHANGE = "all_to_all"


def passed_along(value, axis, steps):
    count = lax.axis_size(axis)
    initial, last = (max(0, -steps), min(count, count - steps))
    return lax.ppermute(value, axis, [(source, source + steps) for source in range(initial, last)])


def sine_table(box_edge):
    counting = jnp.arange(box_edge, dtype=jnp.float32) + 1.0
    scaling = jnp.sqrt(2.0 / (box_edge + 1.0))
    return scaling * jnp.sin(jnp.pi * counting[:, None] * counting[None, :] / (box_edge + 1.0))


def inverse_symbol(box_edge):
    counting = jnp.arange(box_edge, dtype=jnp.float32) + 1.0
    eigen_one = 4.0 * jnp.sin(jnp.pi * counting / (2.0 * (box_edge + 1.0))) ** 2
    eigen_sum = eigen_one[:, None, None] + eigen_one[None, :, None] + eigen_one[None, None, :]
    return 1.0 / (eigen_sum + screen_shift)


def shift_matrices(offset_diff, box_edge):
    cell = jnp.arange(box_edge, dtype=jnp.int32)
    row_shift = cell[None, None, :] == (cell[None, :, None] - offset_diff[:, 0, None, None])
    plane = jnp.arange(box_edge * box_edge, dtype=jnp.int32)
    out_y = (plane // box_edge)[None, :, None]
    out_z = (plane % box_edge)[None, :, None]
    in_y = (plane // box_edge)[None, None, :]
    in_z = (plane % box_edge)[None, None, :]
    plane_shift = (in_y == out_y - offset_diff[:, 1, None, None]) & (
        in_z == out_z - offset_diff[:, 2, None, None]
    )
    return row_shift.astype(jnp.float32), plane_shift.astype(jnp.bfloat16)


def move_bf16(boxes, row_shift, plane_shift):
    planes = jnp.einsum("pxc,pyc->pxy", boxes, plane_shift, preferred_element_type=jnp.float32)
    return jnp.einsum("pxa,pac->pxc", row_shift, planes, precision=highest)


def unmove_f32(fields, row_shift, plane_shift):
    rows = jnp.einsum("pax,pac->pxc", row_shift, fields, precision=highest)
    high = lax.reduce_precision(rows, exponent_bits=8, mantissa_bits=7)
    rest = rows - high
    middle = lax.reduce_precision(rest, exponent_bits=8, mantissa_bits=7)
    low = rest - middle
    parts = jnp.concatenate([high, middle, low], axis=1).astype(jnp.bfloat16)
    moved = jnp.einsum("pxc,pcy->pxy", parts, plane_shift, preferred_element_type=jnp.float32)
    box_edge = fields.shape[1]
    return (moved[:, :box_edge] + moved[:, box_edge : 2 * box_edge]) + moved[:, 2 * box_edge :]


def solve_boxes(density, sine_rows, plane_sines, symbol):
    count_boxes, box_edge, plane_size = density.shape

    def apply_sines(field_block):
        along_first = jnp.einsum("kx,nxf->nkf", sine_rows, field_block, precision=highest)
        flat_rows = along_first.reshape(count_boxes * box_edge, plane_size)
        along_plane = jnp.dot(
            flat_rows, plane_sines, precision=highest, preferred_element_type=jnp.float32
        )
        return along_plane.reshape(count_boxes, box_edge, plane_size)

    spectrum = apply_sines(density) * symbol
    return apply_sines(spectrum)


def corner_of(orbital, offsets):
    listing = jnp.arange(offsets.shape[0], dtype=jnp.int32)
    chosen = orbital[:, None] == listing[None, :]
    return jnp.sum(jnp.where(chosen[:, :, None], offsets[None, :, :], 0), axis=1, dtype=jnp.int32)


def rows_to_orbitals(fields, rows, count):
    chosen = rows[:, None] == jnp.arange(count, dtype=jnp.int32)[None, :]
    return jnp.sum(
        jnp.where(chosen[:, :, None, None], fields[:, None, :, :], 0.0), axis=0
    )


def local(orbitals, offsets, pair_slots, pair_count):
    orb_dev, box_edge, plane_size = orbitals.shape
    workers = lax.axis_size("wrk")
    group_index = lax.axis_index("grp")
    grp_orbs = orb_dev * workers
    own_set = lax.all_gather(orbitals, "wrk", axis=0, tiled=True)
    upper_set = lax.all_gather(passed_along(orbitals, "grp", -1), "wrk", axis=0, tiled=True)
    group_set = jnp.concatenate([own_set, upper_set], axis=0)

    pair_list = pair_slots[0, 0]
    slot_cap = pair_list.shape[0]
    weights = (jnp.arange(slot_cap, dtype=jnp.int32) < pair_count[0, 0]).astype(jnp.float32)
    left_orb = pair_list[:, 0]
    right_orb = pair_list[:, 1]
    offset_diff = corner_of(right_orb, offsets) - corner_of(left_orb, offsets)
    base = group_index * grp_orbs
    left_row = jnp.clip(left_orb - base, 0, 2 * grp_orbs - 1)
    right_row = jnp.clip(right_orb - base, 0, 2 * grp_orbs - 1)
    left_boxes = jnp.take(group_set, left_row, axis=0)
    right_boxes = jnp.take(group_set, right_row, axis=0)
    row_shift, plane_shift = shift_matrices(offset_diff, box_edge)
    right_field = move_bf16(right_boxes, row_shift, plane_shift)

    sine_rows = sine_table(box_edge)
    plane_sines = (sine_rows[:, None, :, None] * sine_rows[None, :, None, :]).reshape(
        plane_size, plane_size
    )
    symbol = inverse_symbol(box_edge).reshape(box_edge, plane_size)
    left_field = left_boxes.astype(jnp.float32)
    potential = solve_boxes(left_field * right_field, sine_rows, plane_sines, symbol)
    weighted = potential * weights[:, None, None]
    to_left = weighted * right_field
    to_right = unmove_f32(weighted * left_field, row_shift, plane_shift)

    upper = right_row >= grp_orbs
    sent_fields = jnp.where(upper[:, None, None], to_right, 0.0)
    sent_rows = jnp.where(upper, right_row - grp_orbs, 0)
    got_fields = passed_along(sent_fields, "grp", 1)
    got_rows = passed_along(sent_rows, "grp", 1)

    kept_right = jnp.where(upper[:, None, None], 0.0, to_right)
    kept_rows = jnp.where(upper, 0, right_row)
    fields = jnp.concatenate([to_left, kept_right, got_fields], axis=0)
    rows = jnp.concatenate([left_row, kept_rows, got_rows], axis=0)
    combined = rows_to_orbitals(fields, rows, grp_orbs)
    if EXCHANGE == "all_to_all":
        pieces = lax.all_to_all(combined, "wrk", 0, 0, tiled=True)
        return jnp.sum(pieces, axis=0, keepdims=True)
    return lax.psum_scatter(combined, "wrk", scatter_dimension=0, tiled=True)


def solution(mesh):
    return jax.shard_map(
        local,
        mesh=mesh,
        in_specs=(P(("grp", "wrk"), None, None), P(), P("grp", "wrk", None, None), P("grp", "wrk")),
        out_specs=P(("grp", "wrk"), None, None),
        check_vma=False,
    )
```

```python
import jax
import jax.numpy as jnp
from jax import lax
from jax.sharding import PartitionSpec as P

screen_shift = 0.05
highest = lax.Precision.HIGHEST
EXCHANGE = "all_to_all"


def passed_along(value, axis, steps):
    count = lax.axis_size(axis)
    initial, last = (max(0, -steps), min(count, count - steps))
    return lax.ppermute(value, axis, [(source, source + steps) for source in range(initial, last)])


def sine_table(box_edge):
    counting = jnp.arange(box_edge, dtype=jnp.float32) + 1.0
    scaling = jnp.sqrt(2.0 / (box_edge + 1.0))
    return scaling * jnp.sin(jnp.pi * counting[:, None] * counting[None, :] / (box_edge + 1.0))


def inverse_symbol(box_edge):
    counting = jnp.arange(box_edge, dtype=jnp.float32) + 1.0
    eigen_one = 4.0 * jnp.sin(jnp.pi * counting / (2.0 * (box_edge + 1.0))) ** 2
    eigen_sum = eigen_one[:, None, None] + eigen_one[None, :, None] + eigen_one[None, None, :]
    return 1.0 / (eigen_sum + screen_shift)


def shift_matrices(offset_diff, box_edge):
    cell = jnp.arange(box_edge, dtype=jnp.int32)
    row_shift = cell[None, None, :] == (cell[None, :, None] - offset_diff[:, 0, None, None])
    plane = jnp.arange(box_edge * box_edge, dtype=jnp.int32)
    out_y = (plane // box_edge)[None, :, None]
    out_z = (plane % box_edge)[None, :, None]
    in_y = (plane // box_edge)[None, None, :]
    in_z = (plane % box_edge)[None, None, :]
    plane_shift = (in_y == out_y - offset_diff[:, 1, None, None]) & (
        in_z == out_z - offset_diff[:, 2, None, None]
    )
    return row_shift.astype(jnp.float32), plane_shift.astype(jnp.bfloat16)


def move_bf16(boxes, row_shift, plane_shift):
    planes = jnp.einsum("pxc,pyc->pxy", boxes, plane_shift, preferred_element_type=jnp.float32)
    return jnp.einsum("pxa,pac->pxc", row_shift, planes, precision=highest)


def unmove_f32(fields, row_shift, plane_shift):
    rows = jnp.einsum("pax,pac->pxc", row_shift, fields, precision=highest)
    high = lax.reduce_precision(rows, exponent_bits=8, mantissa_bits=7)
    rest = rows - high
    middle = lax.reduce_precision(rest, exponent_bits=8, mantissa_bits=7)
    low = rest - middle
    parts = jnp.concatenate([high, middle, low], axis=1).astype(jnp.bfloat16)
    moved = jnp.einsum("pxc,pcy->pxy", parts, plane_shift, preferred_element_type=jnp.float32)
    box_edge = fields.shape[1]
    return (moved[:, :box_edge] + moved[:, box_edge : 2 * box_edge]) + moved[:, 2 * box_edge :]


def solve_boxes(density, sine_rows, plane_sines, symbol):
    count_boxes, box_edge, plane_size = density.shape

    def apply_sines(field_block):
        along_first = jnp.einsum("kx,nxf->nkf", sine_rows, field_block, precision=highest)
        flat_rows = along_first.reshape(count_boxes * box_edge, plane_size)
        along_plane = jnp.dot(
            flat_rows, plane_sines, precision=highest, preferred_element_type=jnp.float32
        )
        return along_plane.reshape(count_boxes, box_edge, plane_size)

    spectrum = apply_sines(density) * symbol
    return apply_sines(spectrum)


def corner_of(orbital, offsets):
    listing = jnp.arange(offsets.shape[0], dtype=jnp.int32)
    chosen = orbital[:, None] == listing[None, :]
    return jnp.sum(jnp.where(chosen[:, :, None], offsets[None, :, :], 0), axis=1, dtype=jnp.int32)


def rows_to_orbitals(fields, rows, count):
    chosen = (rows[:, None] == jnp.arange(count, dtype=jnp.int32)[None, :]).astype(jnp.float32)
    flat = fields.reshape(fields.shape[0], -1)
    summed = jnp.einsum("po,pf->of", chosen, flat, precision=highest)
    return summed.reshape((count,) + fields.shape[1:])


def local(orbitals, offsets, pair_slots, pair_count):
    orb_dev, box_edge, plane_size = orbitals.shape
    workers = lax.axis_size("wrk")
    group_index = lax.axis_index("grp")
    grp_orbs = orb_dev * workers
    upper_set = passed_along(orbitals, "grp", -1)
    local_set = jnp.stack([orbitals, upper_set], axis=0)
    group_set = lax.all_gather(local_set, "wrk", axis=1, tiled=True)
    group_set = group_set.reshape(2 * grp_orbs, box_edge, plane_size)

    pair_list = pair_slots[0, 0]
    slot_cap = pair_list.shape[0]
    weights = (jnp.arange(slot_cap, dtype=jnp.int32) < pair_count[0, 0]).astype(jnp.float32)
    left_orb = pair_list[:, 0]
    right_orb = pair_list[:, 1]
    offset_diff = corner_of(right_orb, offsets) - corner_of(left_orb, offsets)
    base = group_index * grp_orbs
    left_row = jnp.clip(left_orb - base, 0, 2 * grp_orbs - 1)
    right_row = jnp.clip(right_orb - base, 0, 2 * grp_orbs - 1)
    left_boxes = jnp.take(group_set, left_row, axis=0)
    right_boxes = jnp.take(group_set, right_row, axis=0)
    row_shift, plane_shift = shift_matrices(offset_diff, box_edge)
    right_field = move_bf16(right_boxes, row_shift, plane_shift)

    sine_rows = sine_table(box_edge)
    plane_sines = (sine_rows[:, None, :, None] * sine_rows[None, :, None, :]).reshape(
        plane_size, plane_size
    )
    symbol = inverse_symbol(box_edge).reshape(box_edge, plane_size)
    left_field = left_boxes.astype(jnp.float32)
    potential = solve_boxes(left_field * right_field, sine_rows, plane_sines, symbol)
    weighted = potential * weights[:, None, None]
    to_left = weighted * right_field
    to_right = unmove_f32(weighted * left_field, row_shift, plane_shift)

    upper = right_row >= grp_orbs
    sent_fields = jnp.where(upper[:, None, None], to_right, 0.0)
    sent_rows = jnp.where(upper, right_row - grp_orbs, 0)
    got_fields = passed_along(sent_fields, "grp", 1)
    got_rows = passed_along(sent_rows, "grp", 1)

    kept_right = jnp.where(upper[:, None, None], 0.0, to_right)
    kept_rows = jnp.where(upper, 0, right_row)
    fields = jnp.concatenate([to_left, kept_right], axis=0)
    rows = jnp.concatenate([left_row, kept_rows], axis=0)
    combined = rows_to_orbitals(fields, rows, grp_orbs) + rows_to_orbitals(got_fields, got_rows, grp_orbs)
    if EXCHANGE == "all_to_all":
        pieces = lax.all_to_all(combined, "wrk", 0, 0, tiled=True)
        return jnp.sum(pieces, axis=0, keepdims=True)
    return lax.psum_scatter(combined, "wrk", scatter_dimension=0, tiled=True)


def solution(mesh):
    return jax.shard_map(
        local,
        mesh=mesh,
        in_specs=(P(("grp", "wrk"), None, None), P(), P("grp", "wrk", None, None), P("grp", "wrk")),
        out_specs=P(("grp", "wrk"), None, None),
        check_vma=False,
    )
```

```python
import jax
import jax.numpy as jnp
from jax import lax
from jax.sharding import PartitionSpec as P

screen_shift = 0.05
highest = lax.Precision.HIGHEST
EXCHANGE = "all_to_all"


def passed_along(value, axis, steps):
    count = lax.axis_size(axis)
    initial, last = (max(0, -steps), min(count, count - steps))
    return lax.ppermute(value, axis, [(source, source + steps) for source in range(initial, last)])


def sine_table(box_edge):
    counting = jnp.arange(box_edge, dtype=jnp.float32) + 1.0
    scaling = jnp.sqrt(2.0 / (box_edge + 1.0))
    return scaling * jnp.sin(jnp.pi * counting[:, None] * counting[None, :] / (box_edge + 1.0))


def inverse_symbol(box_edge):
    counting = jnp.arange(box_edge, dtype=jnp.float32) + 1.0
    eigen_one = 4.0 * jnp.sin(jnp.pi * counting / (2.0 * (box_edge + 1.0))) ** 2
    eigen_sum = eigen_one[:, None, None] + eigen_one[None, :, None] + eigen_one[None, None, :]
    return 1.0 / (eigen_sum + screen_shift)


def shift_matrices(offset_diff, box_edge):
    cell = jnp.arange(box_edge, dtype=jnp.int32)
    row_shift = cell[None, None, :] == (cell[None, :, None] - offset_diff[:, 0, None, None])
    plane = jnp.arange(box_edge * box_edge, dtype=jnp.int32)
    out_y = (plane // box_edge)[None, :, None]
    out_z = (plane % box_edge)[None, :, None]
    in_y = (plane // box_edge)[None, None, :]
    in_z = (plane % box_edge)[None, None, :]
    plane_shift = (in_y == out_y - offset_diff[:, 1, None, None]) & (
        in_z == out_z - offset_diff[:, 2, None, None]
    )
    return row_shift.astype(jnp.float32), plane_shift.astype(jnp.bfloat16)


def move_bf16(boxes, row_shift, plane_shift):
    planes = jnp.einsum("pxc,pyc->pxy", boxes, plane_shift, preferred_element_type=jnp.float32)
    return jnp.einsum("pxa,pac->pxc", row_shift, planes, precision=highest)


def unmove_f32(fields, row_shift, plane_shift):
    rows = jnp.einsum("pax,pac->pxc", row_shift, fields, precision=highest)
    high = lax.reduce_precision(rows, exponent_bits=8, mantissa_bits=7)
    rest = rows - high
    middle = lax.reduce_precision(rest, exponent_bits=8, mantissa_bits=7)
    low = rest - middle
    parts = jnp.concatenate([high, middle, low], axis=1).astype(jnp.bfloat16)
    moved = jnp.einsum("pxc,pcy->pxy", parts, plane_shift, preferred_element_type=jnp.float32)
    box_edge = fields.shape[1]
    return (moved[:, :box_edge] + moved[:, box_edge : 2 * box_edge]) + moved[:, 2 * box_edge :]


def solve_boxes(density, sine_rows, plane_sines, symbol):
    count_boxes, box_edge, plane_size = density.shape

    def apply_sines(field_block):
        along_first = jnp.einsum("kx,nxf->nkf", sine_rows, field_block, precision=highest)
        flat_rows = along_first.reshape(count_boxes * box_edge, plane_size)
        along_plane = jnp.dot(
            flat_rows, plane_sines, precision=highest, preferred_element_type=jnp.float32
        )
        return along_plane.reshape(count_boxes, box_edge, plane_size)

    spectrum = apply_sines(density) * symbol
    return apply_sines(spectrum)


def corner_of(orbital, offsets):
    listing = jnp.arange(offsets.shape[0], dtype=jnp.int32)
    chosen = orbital[:, None] == listing[None, :]
    return jnp.sum(jnp.where(chosen[:, :, None], offsets[None, :, :], 0), axis=1, dtype=jnp.int32)


def rows_to_orbitals(fields, rows, count):
    chosen = (rows[:, None] == jnp.arange(count, dtype=jnp.int32)[None, :]).astype(jnp.float32)
    flat = fields.reshape(fields.shape[0], -1)
    summed = jnp.einsum("po,pf->of", chosen, flat, precision=highest)
    return summed.reshape((count,) + fields.shape[1:])


def table_lanes(pair_slots, pair_count, box_edge, lanes):
    values = jnp.concatenate([pair_slots[0, 0].reshape(-1), pair_count[0, 0].reshape(1)])
    digits = jnp.concatenate([values // box_edge, values % box_edge]).astype(jnp.bfloat16)
    row = jnp.zeros((lanes,), jnp.bfloat16).at[: digits.shape[0]].set(digits)
    first = (jnp.arange(box_edge, dtype=jnp.int32) == 0)[:, None]
    return jnp.where(first, row[None, :], jnp.zeros((), jnp.bfloat16))[None]


def local(orbitals, offsets, pair_slots, pair_count):
    orb_dev, box_edge, plane_size = orbitals.shape
    workers = lax.axis_size("wrk")
    group_index = lax.axis_index("grp")
    worker_index = lax.axis_index("wrk")
    grp_orbs = orb_dev * workers
    lanes = 128
    slot_cap = pair_slots.shape[2]
    table = table_lanes(pair_slots, pair_count, box_edge, lanes)
    upper_set = passed_along(orbitals, "grp", -1)
    own_part = jnp.concatenate([orbitals, table], axis=-1)
    upper_part = jnp.concatenate([upper_set, jnp.zeros_like(table)], axis=-1)
    local_set = jnp.stack([own_part, upper_part], axis=0)
    gathered = lax.all_gather(local_set, "wrk", axis=1, tiled=True)
    group_set = gathered.reshape(2 * grp_orbs, box_edge, plane_size + lanes)

    entries = 2 * slot_cap + 1
    digits = gathered[0, :, 0, plane_size : plane_size + 2 * entries].astype(jnp.int32)
    values = digits[:, :entries] * box_edge + digits[:, entries:]
    group_slots = values[:, : 2 * slot_cap].reshape(-1, 2)
    group_count = values[:, 2 * slot_cap]
    per_worker = (slot_cap + 1) // 2
    in_use = (jnp.arange(slot_cap, dtype=jnp.int32)[None, :] < group_count[:, None]).reshape(-1)
    rank = jnp.cumsum(in_use.astype(jnp.int32)) - 1
    wanted = worker_index * per_worker + jnp.arange(per_worker, dtype=jnp.int32)
    match = in_use[None, :] & (rank[None, :] == wanted[:, None])
    pair_list = jnp.sum(jnp.where(match[:, :, None], group_slots[None, :, :], 0), axis=1)
    weights = jnp.any(match, axis=1).astype(jnp.float32)

    base = group_index * grp_orbs
    left_orb = jnp.where(weights > 0, pair_list[:, 0], base)
    right_orb = jnp.where(weights > 0, pair_list[:, 1], base)
    offset_diff = corner_of(right_orb, offsets) - corner_of(left_orb, offsets)
    left_row = jnp.clip(left_orb - base, 0, 2 * grp_orbs - 1)
    right_row = jnp.clip(right_orb - base, 0, 2 * grp_orbs - 1)
    left_boxes = jnp.take(group_set, left_row, axis=0)[:, :, :plane_size]
    right_boxes = jnp.take(group_set, right_row, axis=0)[:, :, :plane_size]
    row_shift, plane_shift = shift_matrices(offset_diff, box_edge)
    right_field = move_bf16(right_boxes, row_shift, plane_shift)

    sine_rows = sine_table(box_edge)
    plane_sines = (sine_rows[:, None, :, None] * sine_rows[None, :, None, :]).reshape(
        plane_size, plane_size
    )
    symbol = inverse_symbol(box_edge).reshape(box_edge, plane_size)
    left_field = left_boxes.astype(jnp.float32)
    potential = solve_boxes(left_field * right_field, sine_rows, plane_sines, symbol)
    weighted = potential * weights[:, None, None]
    to_left = weighted * right_field
    to_right = unmove_f32(weighted * left_field, row_shift, plane_shift)

    upper = right_row >= grp_orbs
    sent_fields = jnp.where(upper[:, None, None], to_right, 0.0)
    sent_rows = jnp.where(upper, right_row - grp_orbs, 0)
    got_fields = passed_along(sent_fields, "grp", 1)
    got_rows = passed_along(sent_rows, "grp", 1)

    kept_right = jnp.where(upper[:, None, None], 0.0, to_right)
    kept_rows = jnp.where(upper, 0, right_row)
    fields = jnp.concatenate([to_left, kept_right], axis=0)
    rows = jnp.concatenate([left_row, kept_rows], axis=0)
    combined = rows_to_orbitals(fields, rows, grp_orbs) + rows_to_orbitals(got_fields, got_rows, grp_orbs)
    if EXCHANGE == "all_to_all":
        pieces = lax.all_to_all(combined, "wrk", 0, 0, tiled=True)
        return jnp.sum(pieces, axis=0, keepdims=True)
    return lax.psum_scatter(combined, "wrk", scatter_dimension=0, tiled=True)


def solution(mesh):
    return jax.shard_map(
        local,
        mesh=mesh,
        in_specs=(P(("grp", "wrk"), None, None), P(), P("grp", "wrk", None, None), P("grp", "wrk")),
        out_specs=P(("grp", "wrk"), None, None),
        check_vma=False,
    )
```

```python
import jax
import jax.numpy as jnp
from jax import lax
from jax.sharding import PartitionSpec as P

screen_shift = 0.05
highest = lax.Precision.HIGHEST
WORKER_AXES = ("yx", "core")


def passed_along(value, axis, steps):
    count = lax.axis_size(axis)
    initial, last = (max(0, -steps), min(count, count - steps))
    return lax.ppermute(value, axis, [(source, source + steps) for source in range(initial, last)])


def sine_table(box_edge):
    counting = jnp.arange(box_edge, dtype=jnp.float32) + 1.0
    scaling = jnp.sqrt(2.0 / (box_edge + 1.0))
    return scaling * jnp.sin(jnp.pi * counting[:, None] * counting[None, :] / (box_edge + 1.0))


def inverse_symbol(box_edge):
    counting = jnp.arange(box_edge, dtype=jnp.float32) + 1.0
    eigen_one = 4.0 * jnp.sin(jnp.pi * counting / (2.0 * (box_edge + 1.0))) ** 2
    eigen_sum = eigen_one[:, None, None] + eigen_one[None, :, None] + eigen_one[None, None, :]
    return 1.0 / (eigen_sum + screen_shift)


def shift_matrices(offset_diff, box_edge):
    cell = jnp.arange(box_edge, dtype=jnp.int32)
    row_shift = cell[None, None, :] == (cell[None, :, None] - offset_diff[:, 0, None, None])
    plane = jnp.arange(box_edge * box_edge, dtype=jnp.int32)
    out_y = (plane // box_edge)[None, :, None]
    out_z = (plane % box_edge)[None, :, None]
    in_y = (plane // box_edge)[None, None, :]
    in_z = (plane % box_edge)[None, None, :]
    plane_shift = (in_y == out_y - offset_diff[:, 1, None, None]) & (
        in_z == out_z - offset_diff[:, 2, None, None]
    )
    return row_shift.astype(jnp.float32), plane_shift.astype(jnp.bfloat16)


def move_bf16(boxes, row_shift, plane_shift):
    planes = jnp.einsum("pxc,pyc->pxy", boxes, plane_shift, preferred_element_type=jnp.float32)
    return jnp.einsum("pxa,pac->pxc", row_shift, planes, precision=highest)


def unmove_f32(fields, row_shift, plane_shift):
    rows = jnp.einsum("pax,pac->pxc", row_shift, fields, precision=highest)
    high = lax.reduce_precision(rows, exponent_bits=8, mantissa_bits=7)
    rest = rows - high
    middle = lax.reduce_precision(rest, exponent_bits=8, mantissa_bits=7)
    low = rest - middle
    parts = jnp.concatenate([high, middle, low], axis=1).astype(jnp.bfloat16)
    moved = jnp.einsum("pxc,pcy->pxy", parts, plane_shift, preferred_element_type=jnp.float32)
    box_edge = fields.shape[1]
    return (moved[:, :box_edge] + moved[:, box_edge : 2 * box_edge]) + moved[:, 2 * box_edge :]


def solve_boxes(density, sine_rows, plane_sines, symbol):
    count_boxes, box_edge, plane_size = density.shape

    def apply_sines(field_block):
        along_first = jnp.einsum("kx,nxf->nkf", sine_rows, field_block, precision=highest)
        flat_rows = along_first.reshape(count_boxes * box_edge, plane_size)
        along_plane = jnp.dot(
            flat_rows, plane_sines, precision=highest, preferred_element_type=jnp.float32
        )
        return along_plane.reshape(count_boxes, box_edge, plane_size)

    spectrum = apply_sines(density) * symbol
    return apply_sines(spectrum)


def corner_of(orbital, offsets):
    listing = jnp.arange(offsets.shape[0], dtype=jnp.int32)
    chosen = orbital[:, None] == listing[None, :]
    return jnp.sum(jnp.where(chosen[:, :, None], offsets[None, :, :], 0), axis=1, dtype=jnp.int32)


def rows_to_orbitals(fields, rows, count):
    chosen = (rows[:, None] == jnp.arange(count, dtype=jnp.int32)[None, :]).astype(jnp.float32)
    flat = fields.reshape(fields.shape[0], -1)
    summed = jnp.einsum("po,pf->of", chosen, flat, precision=highest)
    return summed.reshape((count,) + fields.shape[1:])


def table_lanes(pair_slots, pair_count, box_edge, lanes):
    values = jnp.concatenate([pair_slots[0, 0].reshape(-1), pair_count[0, 0].reshape(1)])
    digits = jnp.concatenate([values // box_edge, values % box_edge]).astype(jnp.bfloat16)
    row = jnp.zeros((lanes,), jnp.bfloat16).at[: digits.shape[0]].set(digits)
    first = (jnp.arange(box_edge, dtype=jnp.int32) == 0)[:, None]
    return jnp.where(first, row[None, :], jnp.zeros((), jnp.bfloat16))[None]


def local(orbitals, offsets, pair_slots, pair_count):
    orb_dev, box_edge, plane_size = orbitals.shape
    workers = lax.axis_size("yx") * lax.axis_size("core")
    group_index = lax.axis_index("grp")
    core = lax.axis_index("core")
    worker_index = lax.axis_index("yx") * lax.axis_size("core") + core
    grp_orbs = orb_dev * workers
    lanes = 128
    slot_cap = pair_slots.shape[2]
    table = table_lanes(pair_slots, pair_count, box_edge, lanes)
    upper_set = passed_along(orbitals, "grp", -1)
    own_part = jnp.concatenate([orbitals, table], axis=-1)
    upper_part = jnp.concatenate([upper_set, jnp.zeros_like(table)], axis=-1)
    local_set = jnp.stack([own_part, upper_part], axis=0)
    gathered = lax.all_gather(local_set, WORKER_AXES, axis=1, tiled=True)
    group_set = gathered.reshape(2 * grp_orbs, box_edge, plane_size + lanes)

    entries = 2 * slot_cap + 1
    digits = gathered[0, :, 0, plane_size : plane_size + 2 * entries].astype(jnp.int32)
    values = digits[:, :entries] * box_edge + digits[:, entries:]
    group_slots = values[:, : 2 * slot_cap].reshape(-1, 2)
    group_count = values[:, 2 * slot_cap]
    per_worker = (slot_cap + 1) // 2
    in_use = (jnp.arange(slot_cap, dtype=jnp.int32)[None, :] < group_count[:, None]).reshape(-1)
    rank = jnp.cumsum(in_use.astype(jnp.int32)) - 1
    wanted = worker_index * per_worker + jnp.arange(per_worker, dtype=jnp.int32)
    match = in_use[None, :] & (rank[None, :] == wanted[:, None])
    pair_list = jnp.sum(jnp.where(match[:, :, None], group_slots[None, :, :], 0), axis=1)
    weights = jnp.any(match, axis=1).astype(jnp.float32)

    base = group_index * grp_orbs
    left_orb = jnp.where(weights > 0, pair_list[:, 0], base)
    right_orb = jnp.where(weights > 0, pair_list[:, 1], base)
    offset_diff = corner_of(right_orb, offsets) - corner_of(left_orb, offsets)
    left_row = jnp.clip(left_orb - base, 0, 2 * grp_orbs - 1)
    right_row = jnp.clip(right_orb - base, 0, 2 * grp_orbs - 1)
    both_boxes = jnp.take(group_set, jnp.concatenate([left_row, right_row]), axis=0)[:, :, :plane_size]
    left_boxes = both_boxes[:per_worker]
    right_boxes = both_boxes[per_worker:]
    row_shift, plane_shift = shift_matrices(offset_diff, box_edge)
    right_field = move_bf16(right_boxes, row_shift, plane_shift)

    sine_rows = sine_table(box_edge)
    plane_sines = (sine_rows[:, None, :, None] * sine_rows[None, :, None, :]).reshape(
        plane_size, plane_size
    )
    symbol = inverse_symbol(box_edge).reshape(box_edge, plane_size)
    left_field = left_boxes.astype(jnp.float32)
    potential = solve_boxes(left_field * right_field, sine_rows, plane_sines, symbol)
    weighted = potential * weights[:, None, None]
    to_left = weighted * right_field
    to_right = unmove_f32(weighted * left_field, row_shift, plane_shift)

    upper = right_row >= grp_orbs
    sent_fields = jnp.where(upper[:, None, None], to_right, 0.0)
    sent_rows = jnp.where(upper, right_row - grp_orbs, 0)
    got_fields = passed_along(sent_fields, "grp", 1)
    got_rows = passed_along(sent_rows, "grp", 1)

    kept_right = jnp.where(upper[:, None, None], 0.0, to_right)
    kept_rows = jnp.where(upper, 0, right_row)
    fields = jnp.concatenate([to_left, kept_right], axis=0)
    rows = jnp.concatenate([left_row, kept_rows], axis=0)
    combined = rows_to_orbitals(fields, rows, grp_orbs) + rows_to_orbitals(got_fields, got_rows, grp_orbs)
    cores = lax.axis_size("core")
    by_core = combined.reshape((workers // cores, cores) + combined.shape[1:])
    mine = lax.dynamic_index_in_dim(by_core, core, axis=1, keepdims=False)
    theirs = lax.dynamic_index_in_dim(by_core, cores - 1 - core, axis=1, keepdims=False)
    half = mine + lax.ppermute(theirs, "core", [(0, 1), (1, 0)])
    pieces = lax.all_to_all(half, "yx", 0, 0, tiled=True)
    return jnp.sum(pieces, axis=0, keepdims=True)


def solution(mesh):
    groups, workers = mesh.devices.shape
    split = jax.sharding.Mesh(mesh.devices.reshape(groups, workers // 2, 2), ("grp", "yx", "core"))
    return jax.shard_map(
        local,
        mesh=split,
        in_specs=(
            P(("grp",) + WORKER_AXES, None, None),
            P(),
            P("grp", WORKER_AXES, None, None),
            P("grp", WORKER_AXES),
        ),
        out_specs=P(("grp",) + WORKER_AXES, None, None),
        check_vma=False,
    )
```

```python
import jax
import jax.numpy as jnp
from jax import lax
from jax.sharding import PartitionSpec as P

screen_shift = 0.05
highest = lax.Precision.HIGHEST
WORKER_AXES = ("yx", "core")


def passed_along(value, axis, steps):
    count = lax.axis_size(axis)
    initial, last = (max(0, -steps), min(count, count - steps))
    return lax.ppermute(value, axis, [(source, source + steps) for source in range(initial, last)])


def sine_table(box_edge):
    counting = jnp.arange(box_edge, dtype=jnp.float32) + 1.0
    scaling = jnp.sqrt(2.0 / (box_edge + 1.0))
    return scaling * jnp.sin(jnp.pi * counting[:, None] * counting[None, :] / (box_edge + 1.0))


def inverse_symbol(box_edge):
    counting = jnp.arange(box_edge, dtype=jnp.float32) + 1.0
    eigen_one = 4.0 * jnp.sin(jnp.pi * counting / (2.0 * (box_edge + 1.0))) ** 2
    eigen_sum = eigen_one[:, None, None] + eigen_one[None, :, None] + eigen_one[None, None, :]
    return 1.0 / (eigen_sum + screen_shift)


def shift_matrices(offset_diff, box_edge):
    cell = jnp.arange(box_edge, dtype=jnp.int32)
    row_shift = cell[None, None, :] == (cell[None, :, None] - offset_diff[:, 0, None, None])
    plane = jnp.arange(box_edge * box_edge, dtype=jnp.int32)
    out_y = (plane // box_edge)[None, :, None]
    out_z = (plane % box_edge)[None, :, None]
    in_y = (plane // box_edge)[None, None, :]
    in_z = (plane % box_edge)[None, None, :]
    plane_shift = (in_y == out_y - offset_diff[:, 1, None, None]) & (
        in_z == out_z - offset_diff[:, 2, None, None]
    )
    return row_shift.astype(jnp.float32), plane_shift.astype(jnp.bfloat16)


def move_bf16(boxes, row_shift, plane_shift):
    planes = jnp.einsum("pxc,pyc->pxy", boxes, plane_shift, preferred_element_type=jnp.float32)
    return jnp.einsum("pxa,pac->pxc", row_shift, planes, precision=highest)


def unmove_f32(fields, row_shift, plane_shift):
    rows = jnp.einsum("pax,pac->pxc", row_shift, fields, precision=highest)
    high = lax.reduce_precision(rows, exponent_bits=8, mantissa_bits=7)
    rest = rows - high
    middle = lax.reduce_precision(rest, exponent_bits=8, mantissa_bits=7)
    low = rest - middle
    parts = jnp.concatenate([high, middle, low], axis=1).astype(jnp.bfloat16)
    moved = jnp.einsum("pxc,pcy->pxy", parts, plane_shift, preferred_element_type=jnp.float32)
    box_edge = fields.shape[1]
    return (moved[:, :box_edge] + moved[:, box_edge : 2 * box_edge]) + moved[:, 2 * box_edge :]


def solve_boxes(density, sine_rows, plane_sines, symbol):
    count_boxes, box_edge, plane_size = density.shape

    def apply_sines(field_block):
        along_first = jnp.einsum("kx,nxf->nkf", sine_rows, field_block, precision=highest)
        flat_rows = along_first.reshape(count_boxes * box_edge, plane_size)
        along_plane = jnp.dot(
            flat_rows, plane_sines, precision=highest, preferred_element_type=jnp.float32
        )
        return along_plane.reshape(count_boxes, box_edge, plane_size)

    spectrum = apply_sines(density) * symbol
    return apply_sines(spectrum)


def corner_of(orbital, offsets):
    listing = jnp.arange(offsets.shape[0], dtype=jnp.int32)
    chosen = orbital[:, None] == listing[None, :]
    return jnp.sum(jnp.where(chosen[:, :, None], offsets[None, :, :], 0), axis=1, dtype=jnp.int32)


def rows_to_orbitals(fields, rows, count):
    chosen = (rows[:, None] == jnp.arange(count, dtype=jnp.int32)[None, :]).astype(jnp.float32)
    flat = fields.reshape(fields.shape[0], -1)
    summed = jnp.einsum("po,pf->of", chosen, flat, precision=highest)
    return summed.reshape((count,) + fields.shape[1:])


def table_lanes(pair_slots, pair_count, box_edge, lanes):
    values = jnp.concatenate([pair_slots[0, 0].reshape(-1), pair_count[0, 0].reshape(1)])
    digits = jnp.concatenate([values // box_edge, values % box_edge]).astype(jnp.bfloat16)
    row = jnp.zeros((lanes,), jnp.bfloat16).at[: digits.shape[0]].set(digits)
    first = (jnp.arange(box_edge, dtype=jnp.int32) == 0)[:, None]
    return jnp.where(first, row[None, :], jnp.zeros((), jnp.bfloat16))[None]


def local(orbitals, offsets, pair_slots, pair_count):
    orb_dev, box_edge, plane_size = orbitals.shape
    workers = lax.axis_size("yx") * lax.axis_size("core")
    group_index = lax.axis_index("grp")
    core = lax.axis_index("core")
    worker_index = lax.axis_index("yx") * lax.axis_size("core") + core
    grp_orbs = orb_dev * workers
    lanes = 128
    slot_cap = pair_slots.shape[2]
    table = table_lanes(pair_slots, pair_count, box_edge, lanes)
    upper_set = passed_along(orbitals, "grp", -1)
    own_part = jnp.concatenate([orbitals, table], axis=-1)
    upper_part = jnp.concatenate([upper_set, jnp.zeros_like(table)], axis=-1)
    local_set = jnp.stack([own_part, upper_part], axis=0)
    gathered = lax.all_gather(local_set, WORKER_AXES, axis=1, tiled=True)
    group_set = gathered.reshape(2 * grp_orbs, box_edge, plane_size + lanes)

    entries = 2 * slot_cap + 1
    digits = gathered[0, :, 0, plane_size : plane_size + 2 * entries].astype(jnp.int32)
    values = digits[:, :entries] * box_edge + digits[:, entries:]
    group_slots = values[:, : 2 * slot_cap].reshape(-1, 2)
    group_count = values[:, 2 * slot_cap]
    per_worker = (slot_cap + 1) // 2
    in_use = (jnp.arange(slot_cap, dtype=jnp.int32)[None, :] < group_count[:, None]).reshape(-1)
    rank = jnp.cumsum(in_use.astype(jnp.int32)) - 1
    wanted = worker_index * per_worker + jnp.arange(per_worker, dtype=jnp.int32)
    match = in_use[None, :] & (rank[None, :] == wanted[:, None])
    pair_list = jnp.sum(jnp.where(match[:, :, None], group_slots[None, :, :], 0), axis=1)
    weights = jnp.any(match, axis=1).astype(jnp.float32)

    base = group_index * grp_orbs
    left_orb = jnp.where(weights > 0, pair_list[:, 0], base)
    right_orb = jnp.where(weights > 0, pair_list[:, 1], base)
    offset_diff = corner_of(right_orb, offsets) - corner_of(left_orb, offsets)
    left_row = jnp.clip(left_orb - base, 0, 2 * grp_orbs - 1)
    right_row = jnp.clip(right_orb - base, 0, 2 * grp_orbs - 1)
    both_boxes = jnp.take(group_set, jnp.concatenate([left_row, right_row]), axis=0)[:, :, :plane_size]
    left_boxes = both_boxes[:per_worker]
    right_boxes = both_boxes[per_worker:]
    row_shift, plane_shift = shift_matrices(offset_diff, box_edge)
    right_field = move_bf16(right_boxes, row_shift, plane_shift)

    sine_rows = sine_table(box_edge)
    plane_sines = (sine_rows[:, None, :, None] * sine_rows[None, :, None, :]).reshape(
        plane_size, plane_size
    )
    symbol = inverse_symbol(box_edge).reshape(box_edge, plane_size)
    left_field = left_boxes.astype(jnp.float32)
    potential = solve_boxes(left_field * right_field, sine_rows, plane_sines, symbol)
    weighted = potential * weights[:, None, None]
    to_left = weighted * right_field
    to_right = unmove_f32(weighted * left_field, row_shift, plane_shift)

    upper = right_row >= grp_orbs
    sent_fields = jnp.where(upper[:, None, None], to_right, 0.0)
    sent_rows = jnp.where(upper, right_row - grp_orbs, 0)
    got_fields = passed_along(sent_fields, "grp", 1)
    got_rows = passed_along(sent_rows, "grp", 1)

    kept_right = jnp.where(upper[:, None, None], 0.0, to_right)
    kept_rows = jnp.where(upper, 0, right_row)
    cores = lax.axis_size("core")
    halves = workers // cores

    def add_into(target, fields, rows, on_core):
        keep = (rows % cores) == on_core
        placed = jnp.where(keep[:, None, None], fields, 0.0)
        return target.at[rows // cores].add(placed)

    fields = jnp.concatenate([to_left, kept_right], axis=0)
    rows = jnp.concatenate([left_row, kept_rows], axis=0)
    empty = jnp.zeros((halves, box_edge, plane_size), jnp.float32)
    theirs = add_into(add_into(empty, fields, rows, cores - 1 - core), got_fields, got_rows, cores - 1 - core)
    mine = add_into(add_into(empty, fields, rows, core), got_fields, got_rows, core)
    half = mine + lax.ppermute(theirs, "core", [(0, 1), (1, 0)])
    pieces = lax.all_to_all(half, "yx", 0, 0, tiled=True)
    return jnp.sum(pieces, axis=0, keepdims=True)


def solution(mesh):
    groups, workers = mesh.devices.shape
    split = jax.sharding.Mesh(mesh.devices.reshape(groups, workers // 2, 2), ("grp", "yx", "core"))
    return jax.shard_map(
        local,
        mesh=split,
        in_specs=(
            P(("grp",) + WORKER_AXES, None, None),
            P(),
            P("grp", WORKER_AXES, None, None),
            P("grp", WORKER_AXES),
        ),
        out_specs=P(("grp",) + WORKER_AXES, None, None),
        check_vma=False,
    )
```

```python
import jax
import jax.numpy as jnp
from jax import lax
from jax.sharding import PartitionSpec as P

screen_shift = 0.05
highest = lax.Precision.HIGHEST
WORKER_AXES = ("yx", "core")


def passed_along(value, axis, steps):
    count = lax.axis_size(axis)
    initial, last = (max(0, -steps), min(count, count - steps))
    return lax.ppermute(value, axis, [(source, source + steps) for source in range(initial, last)])


def sine_table(box_edge):
    counting = jnp.arange(box_edge, dtype=jnp.float32) + 1.0
    scaling = jnp.sqrt(2.0 / (box_edge + 1.0))
    return scaling * jnp.sin(jnp.pi * counting[:, None] * counting[None, :] / (box_edge + 1.0))


def inverse_symbol(box_edge):
    counting = jnp.arange(box_edge, dtype=jnp.float32) + 1.0
    eigen_one = 4.0 * jnp.sin(jnp.pi * counting / (2.0 * (box_edge + 1.0))) ** 2
    eigen_sum = eigen_one[:, None, None] + eigen_one[None, :, None] + eigen_one[None, None, :]
    return 1.0 / (eigen_sum + screen_shift)


def shift_matrices(offset_diff, box_edge):
    cell = jnp.arange(box_edge, dtype=jnp.int32)
    row_shift = cell[None, None, :] == (cell[None, :, None] - offset_diff[:, 0, None, None])
    plane = jnp.arange(box_edge * box_edge, dtype=jnp.int32)
    out_y = (plane // box_edge)[None, :, None]
    out_z = (plane % box_edge)[None, :, None]
    in_y = (plane // box_edge)[None, None, :]
    in_z = (plane % box_edge)[None, None, :]
    plane_shift = (in_y == out_y - offset_diff[:, 1, None, None]) & (
        in_z == out_z - offset_diff[:, 2, None, None]
    )
    return row_shift.astype(jnp.float32), plane_shift.astype(jnp.bfloat16)


def move_bf16(boxes, row_shift, plane_shift):
    planes = jnp.einsum("pxc,pyc->pxy", boxes, plane_shift, preferred_element_type=jnp.float32)
    return jnp.einsum("pxa,pac->pxc", row_shift, planes, precision=highest)


def unmove_f32(fields, row_shift, plane_shift):
    rows = jnp.einsum("pax,pac->pxc", row_shift, fields, precision=highest)
    high = lax.reduce_precision(rows, exponent_bits=8, mantissa_bits=7)
    rest = rows - high
    middle = lax.reduce_precision(rest, exponent_bits=8, mantissa_bits=7)
    low = rest - middle
    parts = jnp.concatenate([high, middle, low], axis=1).astype(jnp.bfloat16)
    moved = jnp.einsum("pxc,pcy->pxy", parts, plane_shift, preferred_element_type=jnp.float32)
    box_edge = fields.shape[1]
    return (moved[:, :box_edge] + moved[:, box_edge : 2 * box_edge]) + moved[:, 2 * box_edge :]


def solve_boxes(density, sine_rows, plane_sines, symbol):
    count_boxes, box_edge, plane_size = density.shape

    def apply_sines(field_block):
        along_first = jnp.einsum("kx,nxf->nkf", sine_rows, field_block, precision=highest)
        flat_rows = along_first.reshape(count_boxes * box_edge, plane_size)
        along_plane = jnp.dot(
            flat_rows, plane_sines, precision=highest, preferred_element_type=jnp.float32
        )
        return along_plane.reshape(count_boxes, box_edge, plane_size)

    spectrum = apply_sines(density) * symbol
    return apply_sines(spectrum)


def corner_of(orbital, offsets):
    listing = jnp.arange(offsets.shape[0], dtype=jnp.int32)
    chosen = orbital[:, None] == listing[None, :]
    return jnp.sum(jnp.where(chosen[:, :, None], offsets[None, :, :], 0), axis=1, dtype=jnp.int32)


def rows_to_orbitals(fields, rows, count):
    chosen = (rows[:, None] == jnp.arange(count, dtype=jnp.int32)[None, :]).astype(jnp.float32)
    flat = fields.reshape(fields.shape[0], -1)
    summed = jnp.einsum("po,pf->of", chosen, flat, precision=highest)
    return summed.reshape((count,) + fields.shape[1:])


def table_lanes(pair_slots, pair_count, box_edge, lanes):
    values = jnp.concatenate([pair_slots[0, 0].reshape(-1), pair_count[0, 0].reshape(1)])
    digits = jnp.concatenate([values // box_edge, values % box_edge]).astype(jnp.bfloat16)
    row = jnp.zeros((lanes,), jnp.bfloat16).at[: digits.shape[0]].set(digits)
    first = (jnp.arange(box_edge, dtype=jnp.int32) == 0)[:, None]
    return jnp.where(first, row[None, :], jnp.zeros((), jnp.bfloat16))[None]


def local(orbitals, offsets, pair_slots, pair_count):
    orb_dev, box_edge, plane_size = orbitals.shape
    workers = lax.axis_size("yx") * lax.axis_size("core")
    group_index = lax.axis_index("grp")
    core = lax.axis_index("core")
    worker_index = lax.axis_index("yx") * lax.axis_size("core") + core
    grp_orbs = orb_dev * workers
    lanes = 128
    slot_cap = pair_slots.shape[2]
    table = table_lanes(pair_slots, pair_count, box_edge, lanes)[0]
    cores = lax.axis_size("core")
    chips = lax.axis_size("yx")
    swap = [(0, 1), (1, 0)]
    upper_set = passed_along(orbitals, "grp", -1)
    own_part = jnp.concatenate([orbitals[0], table], axis=-1)
    upper_part = jnp.concatenate([upper_set[0], jnp.zeros_like(table)], axis=-1)
    first = core == 0
    keep = jnp.where(first, own_part, upper_part)
    got = lax.ppermute(jnp.where(first, upper_part, own_part), "core", swap)
    chip_pair = jnp.where(first, jnp.stack([keep, got]), jnp.stack([got, keep]))
    sent = jnp.broadcast_to(chip_pair[None], (chips,) + chip_pair.shape)
    collected = lax.all_to_all(sent, "yx", 0, 0, tiled=True).reshape(
        (grp_orbs, box_edge, plane_size + lanes)
    )
    other = lax.ppermute(collected, "core", swap)

    entries = 2 * slot_cap + 1
    digits = jnp.where(
        first,
        collected[:, 0, plane_size : plane_size + 2 * entries],
        other[:, 0, plane_size : plane_size + 2 * entries],
    ).astype(jnp.int32)
    values = digits[:, :entries] * box_edge + digits[:, entries:]
    group_slots = values[:, : 2 * slot_cap].reshape(-1, 2)
    group_count = values[:, 2 * slot_cap]
    per_worker = (slot_cap + 1) // 2
    in_use = (jnp.arange(slot_cap, dtype=jnp.int32)[None, :] < group_count[:, None]).reshape(-1)
    rank = jnp.cumsum(in_use.astype(jnp.int32)) - 1
    wanted = worker_index * per_worker + jnp.arange(per_worker, dtype=jnp.int32)
    match = in_use[None, :] & (rank[None, :] == wanted[:, None])
    pair_list = jnp.sum(jnp.where(match[:, :, None], group_slots[None, :, :], 0), axis=1)
    weights = jnp.any(match, axis=1).astype(jnp.float32)

    base = group_index * grp_orbs
    left_orb = jnp.where(weights > 0, pair_list[:, 0], base)
    right_orb = jnp.where(weights > 0, pair_list[:, 1], base)
    offset_diff = corner_of(right_orb, offsets) - corner_of(left_orb, offsets)
    left_row = jnp.clip(left_orb - base, 0, 2 * grp_orbs - 1)
    right_row = jnp.clip(right_orb - base, 0, 2 * grp_orbs - 1)
    wanted_rows = jnp.concatenate([left_row, right_row])
    in_collected = (wanted_rows < grp_orbs) == first
    slot = wanted_rows % grp_orbs
    both_boxes = jnp.where(
        in_collected[:, None, None],
        jnp.take(collected, slot, axis=0)[:, :, :plane_size],
        jnp.take(other, slot, axis=0)[:, :, :plane_size],
    )
    left_boxes = both_boxes[:per_worker]
    right_boxes = both_boxes[per_worker:]
    row_shift, plane_shift = shift_matrices(offset_diff, box_edge)
    right_field = move_bf16(right_boxes, row_shift, plane_shift)

    sine_rows = sine_table(box_edge)
    plane_sines = (sine_rows[:, None, :, None] * sine_rows[None, :, None, :]).reshape(
        plane_size, plane_size
    )
    symbol = inverse_symbol(box_edge).reshape(box_edge, plane_size)
    left_field = left_boxes.astype(jnp.float32)
    potential = solve_boxes(left_field * right_field, sine_rows, plane_sines, symbol)
    weighted = potential * weights[:, None, None]
    to_left = weighted * right_field
    to_right = unmove_f32(weighted * left_field, row_shift, plane_shift)

    upper = right_row >= grp_orbs
    sent_fields = jnp.where(upper[:, None, None], to_right, 0.0)
    sent_rows = jnp.where(upper, right_row - grp_orbs, 0)
    got_fields = passed_along(sent_fields, "grp", 1)
    got_rows = passed_along(sent_rows, "grp", 1)

    kept_right = jnp.where(upper[:, None, None], 0.0, to_right)
    kept_rows = jnp.where(upper, 0, right_row)
    halves = workers // cores

    def add_into(target, fields, rows, on_core):
        keep = (rows % cores) == on_core
        placed = jnp.where(keep[:, None, None], fields, 0.0)
        return target.at[rows // cores].add(placed)

    fields = jnp.concatenate([to_left, kept_right], axis=0)
    rows = jnp.concatenate([left_row, kept_rows], axis=0)
    empty = jnp.zeros((halves, box_edge, plane_size), jnp.float32)
    theirs = add_into(add_into(empty, fields, rows, cores - 1 - core), got_fields, got_rows, cores - 1 - core)
    mine = add_into(add_into(empty, fields, rows, core), got_fields, got_rows, core)
    half = mine + lax.ppermute(theirs, "core", [(0, 1), (1, 0)])
    pieces = lax.all_to_all(half, "yx", 0, 0, tiled=True)
    return jnp.sum(pieces, axis=0, keepdims=True)


def solution(mesh):
    groups, workers = mesh.devices.shape
    split = jax.sharding.Mesh(mesh.devices.reshape(groups, workers // 2, 2), ("grp", "yx", "core"))
    return jax.shard_map(
        local,
        mesh=split,
        in_specs=(
            P(("grp",) + WORKER_AXES, None, None),
            P(),
            P("grp", WORKER_AXES, None, None),
            P("grp", WORKER_AXES),
        ),
        out_specs=P(("grp",) + WORKER_AXES, None, None),
        check_vma=False,
    )
```

```python
import jax
import jax.numpy as jnp
from jax import lax
from jax.sharding import PartitionSpec as P

screen_shift = 0.05
highest = lax.Precision.HIGHEST
WORKER_AXES = ("yx", "core")


def passed_along(value, axis, steps):
    count = lax.axis_size(axis)
    initial, last = (max(0, -steps), min(count, count - steps))
    return lax.ppermute(value, axis, [(source, source + steps) for source in range(initial, last)])


def sine_table(box_edge):
    counting = jnp.arange(box_edge, dtype=jnp.float32) + 1.0
    scaling = jnp.sqrt(2.0 / (box_edge + 1.0))
    return scaling * jnp.sin(jnp.pi * counting[:, None] * counting[None, :] / (box_edge + 1.0))


def inverse_symbol(box_edge):
    counting = jnp.arange(box_edge, dtype=jnp.float32) + 1.0
    eigen_one = 4.0 * jnp.sin(jnp.pi * counting / (2.0 * (box_edge + 1.0))) ** 2
    eigen_sum = eigen_one[:, None, None] + eigen_one[None, :, None] + eigen_one[None, None, :]
    return 1.0 / (eigen_sum + screen_shift)


def shift_matrices(offset_diff, box_edge):
    cell = jnp.arange(box_edge, dtype=jnp.int32)
    row_shift = cell[None, None, :] == (cell[None, :, None] - offset_diff[:, 0, None, None])
    plane = jnp.arange(box_edge * box_edge, dtype=jnp.int32)
    out_y = (plane // box_edge)[None, :, None]
    out_z = (plane % box_edge)[None, :, None]
    in_y = (plane // box_edge)[None, None, :]
    in_z = (plane % box_edge)[None, None, :]
    plane_shift = (in_y == out_y - offset_diff[:, 1, None, None]) & (
        in_z == out_z - offset_diff[:, 2, None, None]
    )
    return row_shift.astype(jnp.float32), plane_shift.astype(jnp.bfloat16)


def move_bf16(boxes, row_shift, plane_shift):
    planes = jnp.einsum("pxc,pyc->pxy", boxes, plane_shift, preferred_element_type=jnp.float32)
    return jnp.einsum("pxa,pac->pxc", row_shift, planes, precision=highest)


def unmove_f32(fields, row_shift, plane_shift):
    rows = jnp.einsum("pax,pac->pxc", row_shift, fields, precision=highest)
    high = lax.reduce_precision(rows, exponent_bits=8, mantissa_bits=7)
    rest = rows - high
    middle = lax.reduce_precision(rest, exponent_bits=8, mantissa_bits=7)
    low = rest - middle
    parts = jnp.concatenate([high, middle, low], axis=1).astype(jnp.bfloat16)
    moved = jnp.einsum("pxc,pcy->pxy", parts, plane_shift, preferred_element_type=jnp.float32)
    box_edge = fields.shape[1]
    return (moved[:, :box_edge] + moved[:, box_edge : 2 * box_edge]) + moved[:, 2 * box_edge :]


def plane_table(sine_rows, box_edge):
    plane = jnp.arange(box_edge * box_edge, dtype=jnp.int32)
    cell = jnp.arange(box_edge, dtype=jnp.int32)

    def spread(pick):
        picked = pick.astype(jnp.float32)
        rows = jnp.dot(picked, sine_rows, precision=highest)
        return jnp.dot(rows, picked.T, precision=highest)

    outer = plane[:, None] // box_edge == cell[None, :]
    inner = plane[:, None] % box_edge == cell[None, :]
    return spread(outer) * spread(inner)


def solve_boxes(density, sine_rows, plane_sines, symbol):
    count_boxes, box_edge, plane_size = density.shape

    def apply_sines(field_block):
        along_first = jnp.einsum("kx,nxf->nkf", sine_rows, field_block, precision=highest)
        flat_rows = along_first.reshape(count_boxes * box_edge, plane_size)
        along_plane = jnp.dot(
            flat_rows, plane_sines, precision=highest, preferred_element_type=jnp.float32
        )
        return along_plane.reshape(count_boxes, box_edge, plane_size)

    spectrum = apply_sines(density) * symbol
    return apply_sines(spectrum)


def corner_of(orbital, offsets):
    listing = jnp.arange(offsets.shape[0], dtype=jnp.int32)
    chosen = orbital[:, None] == listing[None, :]
    return jnp.sum(jnp.where(chosen[:, :, None], offsets[None, :, :], 0), axis=1, dtype=jnp.int32)


def rows_to_orbitals(fields, rows, count):
    chosen = (rows[:, None] == jnp.arange(count, dtype=jnp.int32)[None, :]).astype(jnp.float32)
    flat = fields.reshape(fields.shape[0], -1)
    summed = jnp.einsum("po,pf->of", chosen, flat, precision=highest)
    return summed.reshape((count,) + fields.shape[1:])


def table_lanes(pair_slots, pair_count, box_edge, lanes):
    values = jnp.concatenate([pair_slots[0, 0].reshape(-1), pair_count[0, 0].reshape(1)])
    digits = jnp.concatenate([values // box_edge, values % box_edge]).astype(jnp.bfloat16)
    row = jnp.zeros((lanes,), jnp.bfloat16).at[: digits.shape[0]].set(digits)
    first = (jnp.arange(box_edge, dtype=jnp.int32) == 0)[:, None]
    return jnp.where(first, row[None, :], jnp.zeros((), jnp.bfloat16))[None]


def local(orbitals, offsets, pair_slots, pair_count):
    orb_dev, box_edge, plane_size = orbitals.shape
    workers = lax.axis_size("yx") * lax.axis_size("core")
    group_index = lax.axis_index("grp")
    core = lax.axis_index("core")
    worker_index = lax.axis_index("yx") * lax.axis_size("core") + core
    grp_orbs = orb_dev * workers
    lanes = 128
    slot_cap = pair_slots.shape[2]
    table = table_lanes(pair_slots, pair_count, box_edge, lanes)[0]
    cores = lax.axis_size("core")
    chips = lax.axis_size("yx")
    swap = [(0, 1), (1, 0)]
    upper_set = passed_along(orbitals, "grp", -1)
    own_part = jnp.concatenate([orbitals[0], table], axis=-1)
    upper_part = jnp.concatenate([upper_set[0], jnp.zeros_like(table)], axis=-1)
    first = core == 0
    keep = jnp.where(first, own_part, upper_part)
    got = lax.ppermute(jnp.where(first, upper_part, own_part), "core", swap)
    chip_pair = jnp.where(first, jnp.stack([keep, got]), jnp.stack([got, keep]))
    sent = jnp.broadcast_to(chip_pair[None], (chips,) + chip_pair.shape)
    collected = lax.all_to_all(sent, "yx", 0, 0, tiled=True).reshape(
        (grp_orbs, box_edge, plane_size + lanes)
    )
    other = lax.ppermute(collected, "core", swap)

    entries = 2 * slot_cap + 1
    digits = jnp.where(
        first,
        collected[:, 0, plane_size : plane_size + 2 * entries],
        other[:, 0, plane_size : plane_size + 2 * entries],
    ).astype(jnp.int32)
    values = digits[:, :entries] * box_edge + digits[:, entries:]
    group_slots = values[:, : 2 * slot_cap].reshape(-1, 2)
    group_count = values[:, 2 * slot_cap]
    per_worker = (slot_cap + 1) // 2
    in_use = (jnp.arange(slot_cap, dtype=jnp.int32)[None, :] < group_count[:, None]).reshape(-1)
    rank = jnp.cumsum(in_use.astype(jnp.int32)) - 1
    wanted = worker_index * per_worker + jnp.arange(per_worker, dtype=jnp.int32)
    match = in_use[None, :] & (rank[None, :] == wanted[:, None])
    pair_list = jnp.sum(jnp.where(match[:, :, None], group_slots[None, :, :], 0), axis=1)
    weights = jnp.any(match, axis=1).astype(jnp.float32)

    base = group_index * grp_orbs
    left_orb = jnp.where(weights > 0, pair_list[:, 0], base)
    right_orb = jnp.where(weights > 0, pair_list[:, 1], base)
    offset_diff = corner_of(right_orb, offsets) - corner_of(left_orb, offsets)
    left_row = jnp.clip(left_orb - base, 0, 2 * grp_orbs - 1)
    right_row = jnp.clip(right_orb - base, 0, 2 * grp_orbs - 1)
    wanted_rows = jnp.concatenate([left_row, right_row])
    in_collected = (wanted_rows < grp_orbs) == first
    slot = wanted_rows % grp_orbs
    both_boxes = jnp.where(
        in_collected[:, None, None],
        jnp.take(collected, slot, axis=0)[:, :, :plane_size],
        jnp.take(other, slot, axis=0)[:, :, :plane_size],
    )
    left_boxes = both_boxes[:per_worker]
    right_boxes = both_boxes[per_worker:]
    row_shift, plane_shift = shift_matrices(offset_diff, box_edge)
    right_field = move_bf16(right_boxes, row_shift, plane_shift)

    sine_rows = sine_table(box_edge)
    plane_sines = plane_table(sine_rows, box_edge)
    symbol = inverse_symbol(box_edge).reshape(box_edge, plane_size)
    left_field = left_boxes.astype(jnp.float32)
    potential = solve_boxes(left_field * right_field, sine_rows, plane_sines, symbol)
    weighted = potential * weights[:, None, None]
    to_left = weighted * right_field
    to_right = unmove_f32(weighted * left_field, row_shift, plane_shift)

    upper = right_row >= grp_orbs
    sent_fields = jnp.where(upper[:, None, None], to_right, 0.0)
    sent_rows = jnp.where(upper, right_row - grp_orbs, 0)
    got_fields = passed_along(sent_fields, "grp", 1)
    got_rows = passed_along(sent_rows, "grp", 1)

    kept_right = jnp.where(upper[:, None, None], 0.0, to_right)
    kept_rows = jnp.where(upper, 0, right_row)
    halves = workers // cores

    def add_into(target, fields, rows, on_core):
        keep = (rows % cores) == on_core
        placed = jnp.where(keep[:, None, None], fields, 0.0)
        return target.at[rows // cores].add(placed)

    fields = jnp.concatenate([to_left, kept_right], axis=0)
    rows = jnp.concatenate([left_row, kept_rows], axis=0)
    empty = jnp.zeros((halves, box_edge, plane_size), jnp.float32)
    theirs = add_into(add_into(empty, fields, rows, cores - 1 - core), got_fields, got_rows, cores - 1 - core)
    mine = add_into(add_into(empty, fields, rows, core), got_fields, got_rows, core)
    half = mine + lax.ppermute(theirs, "core", [(0, 1), (1, 0)])
    pieces = lax.all_to_all(half, "yx", 0, 0, tiled=True)
    return jnp.sum(pieces, axis=0, keepdims=True)


def solution(mesh):
    groups, workers = mesh.devices.shape
    split = jax.sharding.Mesh(mesh.devices.reshape(groups, workers // 2, 2), ("grp", "yx", "core"))
    return jax.shard_map(
        local,
        mesh=split,
        in_specs=(
            P(("grp",) + WORKER_AXES, None, None),
            P(),
            P("grp", WORKER_AXES, None, None),
            P("grp", WORKER_AXES),
        ),
        out_specs=P(("grp",) + WORKER_AXES, None, None),
        check_vma=False,
    )
```

```python
import jax
import jax.numpy as jnp
from jax import lax
from jax.sharding import PartitionSpec as P

screen_shift = 0.05
highest = lax.Precision.HIGHEST
WORKER_AXES = ("yx", "core")


def passed_along(value, axis, steps):
    count = lax.axis_size(axis)
    initial, last = (max(0, -steps), min(count, count - steps))
    return lax.ppermute(value, axis, [(source, source + steps) for source in range(initial, last)])


def sine_table(box_edge):
    counting = jnp.arange(box_edge, dtype=jnp.float32) + 1.0
    scaling = jnp.sqrt(2.0 / (box_edge + 1.0))
    return scaling * jnp.sin(jnp.pi * counting[:, None] * counting[None, :] / (box_edge + 1.0))


def inverse_symbol(box_edge):
    counting = jnp.arange(box_edge, dtype=jnp.float32) + 1.0
    eigen_one = 4.0 * jnp.sin(jnp.pi * counting / (2.0 * (box_edge + 1.0))) ** 2
    eigen_sum = eigen_one[:, None, None] + eigen_one[None, :, None] + eigen_one[None, None, :]
    return 1.0 / (eigen_sum + screen_shift)


def shift_matrices(offset_diff, box_edge):
    cell = jnp.arange(box_edge, dtype=jnp.int32)
    row_shift = cell[None, None, :] == (cell[None, :, None] - offset_diff[:, 0, None, None])
    plane = jnp.arange(box_edge * box_edge, dtype=jnp.int32)
    out_y = (plane // box_edge)[None, :, None]
    out_z = (plane % box_edge)[None, :, None]
    in_y = (plane // box_edge)[None, None, :]
    in_z = (plane % box_edge)[None, None, :]
    plane_shift = (in_y == out_y - offset_diff[:, 1, None, None]) & (
        in_z == out_z - offset_diff[:, 2, None, None]
    )
    return row_shift.astype(jnp.float32), plane_shift.astype(jnp.bfloat16)


def move_bf16(boxes, row_shift, plane_shift):
    planes = jnp.einsum("pxc,pyc->pxy", boxes, plane_shift, preferred_element_type=jnp.float32)
    return jnp.einsum("pxa,pac->pxc", row_shift, planes, precision=highest)


def unmove_f32(fields, row_shift, plane_shift):
    rows = jnp.einsum("pax,pac->pxc", row_shift, fields, precision=highest)
    high = lax.reduce_precision(rows, exponent_bits=8, mantissa_bits=7)
    rest = rows - high
    middle = lax.reduce_precision(rest, exponent_bits=8, mantissa_bits=7)
    low = rest - middle
    parts = jnp.concatenate([high, middle, low], axis=1).astype(jnp.bfloat16)
    moved = jnp.einsum("pxc,pcy->pxy", parts, plane_shift, preferred_element_type=jnp.float32)
    box_edge = fields.shape[1]
    return (moved[:, :box_edge] + moved[:, box_edge : 2 * box_edge]) + moved[:, 2 * box_edge :]


def plane_table(sine_rows, box_edge):
    plane = jnp.arange(box_edge * box_edge, dtype=jnp.int32)
    cell = jnp.arange(box_edge, dtype=jnp.int32)

    def spread(pick):
        picked = pick.astype(jnp.float32)
        rows = jnp.dot(picked, sine_rows, precision=highest)
        return jnp.dot(rows, picked.T, precision=highest)

    outer = plane[:, None] // box_edge == cell[None, :]
    inner = plane[:, None] % box_edge == cell[None, :]
    return spread(outer) * spread(inner)


def solve_boxes(density, sine_rows, plane_sines, symbol):
    count_boxes, box_edge, plane_size = density.shape

    def apply_sines(field_block):
        along_first = jnp.einsum("kx,nxf->nkf", sine_rows, field_block, precision=highest)
        flat_rows = along_first.reshape(count_boxes * box_edge, plane_size)
        along_plane = jnp.dot(
            flat_rows, plane_sines, precision=highest, preferred_element_type=jnp.float32
        )
        return along_plane.reshape(count_boxes, box_edge, plane_size)

    spectrum = apply_sines(density) * symbol
    return apply_sines(spectrum)


def corner_of(orbital, offsets):
    listing = jnp.arange(offsets.shape[0], dtype=jnp.int32)
    chosen = orbital[:, None] == listing[None, :]
    return jnp.sum(jnp.where(chosen[:, :, None], offsets[None, :, :], 0), axis=1, dtype=jnp.int32)


def rows_to_orbitals(fields, rows, count):
    chosen = (rows[:, None] == jnp.arange(count, dtype=jnp.int32)[None, :]).astype(jnp.float32)
    flat = fields.reshape(fields.shape[0], -1)
    summed = jnp.einsum("po,pf->of", chosen, flat, precision=highest)
    return summed.reshape((count,) + fields.shape[1:])


def table_lanes(pair_slots, pair_count, box_edge, lanes):
    values = jnp.concatenate([pair_slots[0, 0].reshape(-1), pair_count[0, 0].reshape(1)])
    digits = jnp.concatenate([values // box_edge, values % box_edge]).astype(jnp.bfloat16)
    row = jnp.zeros((lanes,), jnp.bfloat16).at[: digits.shape[0]].set(digits)
    first = (jnp.arange(box_edge, dtype=jnp.int32) == 0)[:, None]
    return jnp.where(first, row[None, :], jnp.zeros((), jnp.bfloat16))[None]


def local(orbitals, offsets, pair_slots, pair_count):
    orb_dev, box_edge, plane_size = orbitals.shape
    workers = lax.axis_size("yx") * lax.axis_size("core")
    group_index = lax.axis_index("grp")
    core = lax.axis_index("core")
    worker_index = lax.axis_index("yx") * lax.axis_size("core") + core
    grp_orbs = orb_dev * workers
    lanes = 128
    slot_cap = pair_slots.shape[2]
    table = table_lanes(pair_slots, pair_count, box_edge, lanes)[0]
    cores = lax.axis_size("core")
    chips = lax.axis_size("yx")
    swap = [(0, 1), (1, 0)]
    groups = lax.axis_size("grp")
    own_part = jnp.concatenate([orbitals[0], table], axis=-1)
    upper_same = passed_along(orbitals, "grp", -1)[0]
    upper_first = lax.ppermute(
        orbitals, ("grp", "core"), [((g + 1) * cores, g * cores + 1) for g in range(groups - 1)]
    )[0]
    own_second = lax.ppermute(own_part, "core", [(1, 0)])
    first = core == 0
    upper_pair = jnp.concatenate(
        [jnp.stack([upper_first, upper_same]), jnp.zeros((2, box_edge, lanes), jnp.bfloat16)], axis=-1
    )
    chip_pair = jnp.where(first, jnp.stack([own_part, own_second]), upper_pair)
    sent = jnp.broadcast_to(chip_pair[None], (chips,) + chip_pair.shape)
    collected = lax.all_to_all(sent, "yx", 0, 0, tiled=True).reshape(
        (grp_orbs, box_edge, plane_size + lanes)
    )
    other = lax.ppermute(collected, "core", swap)

    entries = 2 * slot_cap + 1
    digits = jnp.where(
        first,
        collected[:, 0, plane_size : plane_size + 2 * entries],
        other[:, 0, plane_size : plane_size + 2 * entries],
    ).astype(jnp.int32)
    values = digits[:, :entries] * box_edge + digits[:, entries:]
    group_slots = values[:, : 2 * slot_cap].reshape(-1, 2)
    group_count = values[:, 2 * slot_cap]
    per_worker = (slot_cap + 1) // 2
    in_use = (jnp.arange(slot_cap, dtype=jnp.int32)[None, :] < group_count[:, None]).reshape(-1)
    rank = jnp.cumsum(in_use.astype(jnp.int32)) - 1
    wanted = worker_index * per_worker + jnp.arange(per_worker, dtype=jnp.int32)
    match = in_use[None, :] & (rank[None, :] == wanted[:, None])
    pair_list = jnp.sum(jnp.where(match[:, :, None], group_slots[None, :, :], 0), axis=1)
    weights = jnp.any(match, axis=1).astype(jnp.float32)

    base = group_index * grp_orbs
    left_orb = jnp.where(weights > 0, pair_list[:, 0], base)
    right_orb = jnp.where(weights > 0, pair_list[:, 1], base)
    offset_diff = corner_of(right_orb, offsets) - corner_of(left_orb, offsets)
    left_row = jnp.clip(left_orb - base, 0, 2 * grp_orbs - 1)
    right_row = jnp.clip(right_orb - base, 0, 2 * grp_orbs - 1)
    wanted_rows = jnp.concatenate([left_row, right_row])
    in_collected = (wanted_rows < grp_orbs) == first
    slot = wanted_rows % grp_orbs
    both_boxes = jnp.where(
        in_collected[:, None, None],
        jnp.take(collected, slot, axis=0)[:, :, :plane_size],
        jnp.take(other, slot, axis=0)[:, :, :plane_size],
    )
    left_boxes = both_boxes[:per_worker]
    right_boxes = both_boxes[per_worker:]
    row_shift, plane_shift = shift_matrices(offset_diff, box_edge)
    right_field = move_bf16(right_boxes, row_shift, plane_shift)

    sine_rows = sine_table(box_edge)
    plane_sines = plane_table(sine_rows, box_edge)
    symbol = inverse_symbol(box_edge).reshape(box_edge, plane_size)
    left_field = left_boxes.astype(jnp.float32)
    potential = solve_boxes(left_field * right_field, sine_rows, plane_sines, symbol)
    weighted = potential * weights[:, None, None]
    to_left = weighted * right_field
    to_right = unmove_f32(weighted * left_field, row_shift, plane_shift)

    upper = right_row >= grp_orbs
    sent_fields = jnp.where(upper[:, None, None], to_right, 0.0)
    sent_rows = jnp.where(upper, right_row - grp_orbs, 0)
    got_fields = passed_along(sent_fields, "grp", 1)
    got_rows = passed_along(sent_rows, "grp", 1)

    kept_right = jnp.where(upper[:, None, None], 0.0, to_right)
    kept_rows = jnp.where(upper, 0, right_row)
    halves = workers // cores

    def add_into(target, fields, rows, on_core):
        keep = (rows % cores) == on_core
        placed = jnp.where(keep[:, None, None], fields, 0.0)
        return target.at[rows // cores].add(placed)

    fields = jnp.concatenate([to_left, kept_right], axis=0)
    rows = jnp.concatenate([left_row, kept_rows], axis=0)
    empty = jnp.zeros((halves, box_edge, plane_size), jnp.float32)
    theirs = add_into(add_into(empty, fields, rows, cores - 1 - core), got_fields, got_rows, cores - 1 - core)
    mine = add_into(add_into(empty, fields, rows, core), got_fields, got_rows, core)
    half = mine + lax.ppermute(theirs, "core", [(0, 1), (1, 0)])
    pieces = lax.all_to_all(half, "yx", 0, 0, tiled=True)
    return jnp.sum(pieces, axis=0, keepdims=True)


def solution(mesh):
    groups, workers = mesh.devices.shape
    split = jax.sharding.Mesh(mesh.devices.reshape(groups, workers // 2, 2), ("grp", "yx", "core"))
    return jax.shard_map(
        local,
        mesh=split,
        in_specs=(
            P(("grp",) + WORKER_AXES, None, None),
            P(),
            P("grp", WORKER_AXES, None, None),
            P("grp", WORKER_AXES),
        ),
        out_specs=P(("grp",) + WORKER_AXES, None, None),
        check_vma=False,
    )
```

```python
import jax
import jax.numpy as jnp
from jax import lax
from jax.sharding import PartitionSpec as P

screen_shift = 0.05
highest = lax.Precision.HIGHEST
WORKER_AXES = ("yx", "core")


def passed_along(value, axis, steps):
    count = lax.axis_size(axis)
    initial, last = (max(0, -steps), min(count, count - steps))
    return lax.ppermute(value, axis, [(source, source + steps) for source in range(initial, last)])


def sine_table(box_edge):
    counting = jnp.arange(box_edge, dtype=jnp.float32) + 1.0
    scaling = jnp.sqrt(2.0 / (box_edge + 1.0))
    return scaling * jnp.sin(jnp.pi * counting[:, None] * counting[None, :] / (box_edge + 1.0))


def inverse_symbol(box_edge):
    counting = jnp.arange(box_edge, dtype=jnp.float32) + 1.0
    eigen_one = 4.0 * jnp.sin(jnp.pi * counting / (2.0 * (box_edge + 1.0))) ** 2
    eigen_sum = eigen_one[:, None, None] + eigen_one[None, :, None] + eigen_one[None, None, :]
    return 1.0 / (eigen_sum + screen_shift)


def shift_matrices(offset_diff, box_edge):
    cell = jnp.arange(box_edge, dtype=jnp.int32)
    row_shift = cell[None, None, :] == (cell[None, :, None] - offset_diff[:, 0, None, None])
    plane = jnp.arange(box_edge * box_edge, dtype=jnp.int32)
    out_y = (plane // box_edge)[None, :, None]
    out_z = (plane % box_edge)[None, :, None]
    in_y = (plane // box_edge)[None, None, :]
    in_z = (plane % box_edge)[None, None, :]
    plane_shift = (in_y == out_y - offset_diff[:, 1, None, None]) & (
        in_z == out_z - offset_diff[:, 2, None, None]
    )
    return row_shift.astype(jnp.float32), plane_shift.astype(jnp.bfloat16)


def move_bf16(boxes, row_shift, plane_shift):
    planes = jnp.einsum("pxc,pyc->pxy", boxes, plane_shift, preferred_element_type=jnp.float32)
    return jnp.einsum("pxa,pac->pxc", row_shift, planes, precision=highest)


def unmove_f32(fields, row_shift, plane_shift):
    rows = jnp.einsum("pax,pac->pxc", row_shift, fields, precision=highest)
    high = lax.reduce_precision(rows, exponent_bits=8, mantissa_bits=7)
    rest = rows - high
    middle = lax.reduce_precision(rest, exponent_bits=8, mantissa_bits=7)
    low = rest - middle
    parts = jnp.concatenate([high, middle, low], axis=1).astype(jnp.bfloat16)
    moved = jnp.einsum("pxc,pcy->pxy", parts, plane_shift, preferred_element_type=jnp.float32)
    box_edge = fields.shape[1]
    return (moved[:, :box_edge] + moved[:, box_edge : 2 * box_edge]) + moved[:, 2 * box_edge :]


def plane_table(sine_rows, box_edge):
    plane = jnp.arange(box_edge * box_edge, dtype=jnp.int32)
    cell = jnp.arange(box_edge, dtype=jnp.int32)

    def spread(pick):
        picked = pick.astype(jnp.float32)
        rows = jnp.dot(picked, sine_rows, precision=highest)
        return jnp.dot(rows, picked.T, precision=highest)

    outer = plane[:, None] // box_edge == cell[None, :]
    inner = plane[:, None] % box_edge == cell[None, :]
    return spread(outer) * spread(inner)


def solve_boxes(density, sine_rows, plane_sines, symbol):
    count_boxes, box_edge, plane_size = density.shape

    def apply_sines(field_block):
        along_first = jnp.einsum("kx,nxf->nkf", sine_rows, field_block, precision=highest)
        flat_rows = along_first.reshape(count_boxes * box_edge, plane_size)
        along_plane = jnp.dot(
            flat_rows, plane_sines, precision=highest, preferred_element_type=jnp.float32
        )
        return along_plane.reshape(count_boxes, box_edge, plane_size)

    spectrum = apply_sines(density) * symbol
    return apply_sines(spectrum)


def corner_of(orbital, offsets):
    listing = jnp.arange(offsets.shape[0], dtype=jnp.int32)
    chosen = orbital[:, None] == listing[None, :]
    return jnp.sum(jnp.where(chosen[:, :, None], offsets[None, :, :], 0), axis=1, dtype=jnp.int32)


def rows_to_orbitals(fields, rows, count):
    chosen = (rows[:, None] == jnp.arange(count, dtype=jnp.int32)[None, :]).astype(jnp.float32)
    flat = fields.reshape(fields.shape[0], -1)
    summed = jnp.einsum("po,pf->of", chosen, flat, precision=highest)
    return summed.reshape((count,) + fields.shape[1:])


def table_lanes(pair_slots, pair_count, box_edge, lanes):
    values = jnp.concatenate([pair_slots[0, 0].reshape(-1), pair_count[0, 0].reshape(1)])
    digits = jnp.concatenate([values // box_edge, values % box_edge]).astype(jnp.bfloat16)
    row = jnp.zeros((lanes,), jnp.bfloat16).at[: digits.shape[0]].set(digits)
    first = (jnp.arange(box_edge, dtype=jnp.int32) == 0)[:, None]
    return jnp.where(first, row[None, :], jnp.zeros((), jnp.bfloat16))[None]


def local(orbitals, offsets, pair_slots, pair_count):
    orb_dev, box_edge, plane_size = orbitals.shape
    workers = lax.axis_size("yx") * lax.axis_size("core")
    group_index = lax.axis_index("grp")
    core = lax.axis_index("core")
    worker_index = lax.axis_index("yx") * lax.axis_size("core") + core
    grp_orbs = orb_dev * workers
    lanes = 128
    slot_cap = pair_slots.shape[2]
    table = table_lanes(pair_slots, pair_count, box_edge, lanes)[0]
    cores = lax.axis_size("core")
    chips = lax.axis_size("yx")
    swap = [(0, 1), (1, 0)]
    upper_set = passed_along(orbitals, "grp", -1)
    own_part = jnp.concatenate([orbitals[0], table], axis=-1)
    upper_part = jnp.concatenate([upper_set[0], jnp.zeros_like(table)], axis=-1)
    first = core == 0
    keep = jnp.where(first, own_part, upper_part)
    got = lax.ppermute(jnp.where(first, upper_part, own_part), "core", swap)
    chip_pair = jnp.where(first, jnp.stack([keep, got]), jnp.stack([got, keep]))
    sent = jnp.broadcast_to(chip_pair[None], (chips,) + chip_pair.shape)
    collected = lax.all_to_all(sent, "yx", 0, 0, tiled=True).reshape(
        (grp_orbs, box_edge, plane_size + lanes)
    )
    other = lax.ppermute(collected, "core", swap)

    entries = 2 * slot_cap + 1
    digits = jnp.where(
        first,
        collected[:, 0, plane_size : plane_size + 2 * entries],
        other[:, 0, plane_size : plane_size + 2 * entries],
    ).astype(jnp.int32)
    values = digits[:, :entries] * box_edge + digits[:, entries:]
    group_slots = values[:, : 2 * slot_cap].reshape(-1, 2)
    group_count = values[:, 2 * slot_cap]
    per_worker = (slot_cap + 1) // 2
    in_use = (jnp.arange(slot_cap, dtype=jnp.int32)[None, :] < group_count[:, None]).reshape(-1)
    rank = jnp.cumsum(in_use.astype(jnp.int32)) - 1
    wanted = worker_index * per_worker + jnp.arange(per_worker, dtype=jnp.int32)
    match = in_use[None, :] & (rank[None, :] == wanted[:, None])
    pair_list = jnp.sum(jnp.where(match[:, :, None], group_slots[None, :, :], 0), axis=1)
    weights = jnp.any(match, axis=1).astype(jnp.float32)

    base = group_index * grp_orbs
    left_orb = jnp.where(weights > 0, pair_list[:, 0], base)
    right_orb = jnp.where(weights > 0, pair_list[:, 1], base)
    offset_diff = corner_of(right_orb, offsets) - corner_of(left_orb, offsets)
    left_row = jnp.clip(left_orb - base, 0, 2 * grp_orbs - 1)
    right_row = jnp.clip(right_orb - base, 0, 2 * grp_orbs - 1)
    wanted_rows = jnp.concatenate([left_row, right_row])
    in_collected = (wanted_rows < grp_orbs) == first
    slot = wanted_rows % grp_orbs
    both_boxes = jnp.where(
        in_collected[:, None, None],
        jnp.take(collected, slot, axis=0)[:, :, :plane_size],
        jnp.take(other, slot, axis=0)[:, :, :plane_size],
    )
    left_boxes = both_boxes[:per_worker]
    right_boxes = both_boxes[per_worker:]
    row_shift, plane_shift = shift_matrices(offset_diff, box_edge)
    right_field = move_bf16(right_boxes, row_shift, plane_shift)

    sine_rows = sine_table(box_edge)
    plane_sines = plane_table(sine_rows, box_edge)
    symbol = inverse_symbol(box_edge).reshape(box_edge, plane_size)
    left_field = left_boxes.astype(jnp.float32)
    potential = solve_boxes(left_field * right_field, sine_rows, plane_sines, symbol)
    weighted = potential * weights[:, None, None]
    to_left = weighted * right_field
    to_right = unmove_f32(weighted * left_field, row_shift, plane_shift)

    upper = right_row >= grp_orbs
    sent_fields = jnp.where(upper[:, None, None], to_right, 0.0)
    sent_rows = jnp.where(upper, right_row - grp_orbs, 0)
    row_block = jnp.where(
        (jnp.arange(box_edge)[:, None] == 0) & (jnp.arange(lanes)[None, :] == 0),
        sent_rows[:, None, None].astype(jnp.float32),
        0.0,
    )
    got = passed_along(jnp.concatenate([sent_fields, row_block], axis=-1), "grp", 1)
    got_fields = got[:, :, :plane_size]
    got_rows = got[:, 0, plane_size].astype(jnp.int32)

    kept_right = jnp.where(upper[:, None, None], 0.0, to_right)
    kept_rows = jnp.where(upper, 0, right_row)
    halves = workers // cores

    def add_into(target, fields, rows, on_core):
        keep = (rows % cores) == on_core
        placed = jnp.where(keep[:, None, None], fields, 0.0)
        return target.at[rows // cores].add(placed)

    fields = jnp.concatenate([to_left, kept_right], axis=0)
    rows = jnp.concatenate([left_row, kept_rows], axis=0)
    empty = jnp.zeros((halves, box_edge, plane_size), jnp.float32)
    theirs = add_into(add_into(empty, fields, rows, cores - 1 - core), got_fields, got_rows, cores - 1 - core)
    mine = add_into(add_into(empty, fields, rows, core), got_fields, got_rows, core)
    half = mine + lax.ppermute(theirs, "core", [(0, 1), (1, 0)])
    pieces = lax.all_to_all(half, "yx", 0, 0, tiled=True)
    return jnp.sum(pieces, axis=0, keepdims=True)


def solution(mesh):
    groups, workers = mesh.devices.shape
    split = jax.sharding.Mesh(mesh.devices.reshape(groups, workers // 2, 2), ("grp", "yx", "core"))
    return jax.shard_map(
        local,
        mesh=split,
        in_specs=(
            P(("grp",) + WORKER_AXES, None, None),
            P(),
            P("grp", WORKER_AXES, None, None),
            P("grp", WORKER_AXES),
        ),
        out_specs=P(("grp",) + WORKER_AXES, None, None),
        check_vma=False,
    )
```

```python
import jax
import jax.numpy as jnp
from jax import lax
from jax.sharding import PartitionSpec as P

screen_shift = 0.05
highest = lax.Precision.HIGHEST
WORKER_AXES = ("yx", "core")


def passed_along(value, axis, steps):
    count = lax.axis_size(axis)
    initial, last = (max(0, -steps), min(count, count - steps))
    return lax.ppermute(value, axis, [(source, source + steps) for source in range(initial, last)])


def sine_table(box_edge):
    counting = jnp.arange(box_edge, dtype=jnp.float32) + 1.0
    scaling = jnp.sqrt(2.0 / (box_edge + 1.0))
    return scaling * jnp.sin(jnp.pi * counting[:, None] * counting[None, :] / (box_edge + 1.0))


def inverse_symbol(box_edge):
    counting = jnp.arange(box_edge, dtype=jnp.float32) + 1.0
    eigen_one = 4.0 * jnp.sin(jnp.pi * counting / (2.0 * (box_edge + 1.0))) ** 2
    eigen_sum = eigen_one[:, None, None] + eigen_one[None, :, None] + eigen_one[None, None, :]
    return 1.0 / (eigen_sum + screen_shift)


def shift_matrices(offset_diff, box_edge):
    cell = jnp.arange(box_edge, dtype=jnp.int32)
    row_shift = cell[None, None, :] == (cell[None, :, None] - offset_diff[:, 0, None, None])
    plane = jnp.arange(box_edge * box_edge, dtype=jnp.int32)
    out_y = (plane // box_edge)[None, :, None]
    out_z = (plane % box_edge)[None, :, None]
    in_y = (plane // box_edge)[None, None, :]
    in_z = (plane % box_edge)[None, None, :]
    plane_shift = (in_y == out_y - offset_diff[:, 1, None, None]) & (
        in_z == out_z - offset_diff[:, 2, None, None]
    )
    return row_shift.astype(jnp.float32), plane_shift.astype(jnp.bfloat16)


def move_bf16(boxes, row_shift, plane_shift):
    planes = jnp.einsum("pxc,pyc->pxy", boxes, plane_shift, preferred_element_type=jnp.float32)
    return jnp.einsum("pxa,pac->pxc", row_shift, planes, precision=highest)


def unmove_f32(fields, row_shift, plane_shift):
    rows = jnp.einsum("pax,pac->pxc", row_shift, fields, precision=highest)
    high = lax.reduce_precision(rows, exponent_bits=8, mantissa_bits=7)
    rest = rows - high
    middle = lax.reduce_precision(rest, exponent_bits=8, mantissa_bits=7)
    low = rest - middle
    parts = jnp.concatenate([high, middle, low], axis=1).astype(jnp.bfloat16)
    moved = jnp.einsum("pxc,pcy->pxy", parts, plane_shift, preferred_element_type=jnp.float32)
    box_edge = fields.shape[1]
    return (moved[:, :box_edge] + moved[:, box_edge : 2 * box_edge]) + moved[:, 2 * box_edge :]


def plane_table(sine_rows, box_edge):
    plane = jnp.arange(box_edge * box_edge, dtype=jnp.int32)
    cell = jnp.arange(box_edge, dtype=jnp.int32)

    def spread(pick):
        picked = pick.astype(jnp.float32)
        rows = jnp.dot(picked, sine_rows, precision=highest)
        return jnp.dot(rows, picked.T, precision=highest)

    outer = plane[:, None] // box_edge == cell[None, :]
    inner = plane[:, None] % box_edge == cell[None, :]
    return spread(outer) * spread(inner)


def solve_boxes(density, sine_rows, plane_sines, symbol):
    count_boxes, box_edge, plane_size = density.shape

    def apply_sines(field_block):
        along_first = jnp.einsum("kx,nxf->nkf", sine_rows, field_block, precision=highest)
        flat_rows = along_first.reshape(count_boxes * box_edge, plane_size)
        along_plane = jnp.dot(
            flat_rows, plane_sines, precision=highest, preferred_element_type=jnp.float32
        )
        return along_plane.reshape(count_boxes, box_edge, plane_size)

    spectrum = apply_sines(density) * symbol
    return apply_sines(spectrum)


def corner_of(orbital, offsets):
    listing = jnp.arange(offsets.shape[0], dtype=jnp.int32)
    chosen = orbital[:, None] == listing[None, :]
    return jnp.sum(jnp.where(chosen[:, :, None], offsets[None, :, :], 0), axis=1, dtype=jnp.int32)


def rows_to_orbitals(fields, rows, count):
    chosen = (rows[:, None] == jnp.arange(count, dtype=jnp.int32)[None, :]).astype(jnp.float32)
    flat = fields.reshape(fields.shape[0], -1)
    summed = jnp.einsum("po,pf->of", chosen, flat, precision=highest)
    return summed.reshape((count,) + fields.shape[1:])


def table_lanes(pair_slots, pair_count, box_edge, lanes):
    values = jnp.concatenate([pair_slots[0, 0].reshape(-1), pair_count[0, 0].reshape(1)])
    digits = jnp.concatenate([values // box_edge, values % box_edge]).astype(jnp.bfloat16)
    row = jnp.zeros((lanes,), jnp.bfloat16).at[: digits.shape[0]].set(digits)
    first = (jnp.arange(box_edge, dtype=jnp.int32) == 0)[:, None]
    return jnp.where(first, row[None, :], jnp.zeros((), jnp.bfloat16))[None]


def local(orbitals, offsets, pair_slots, pair_count):
    orb_dev, box_edge, plane_size = orbitals.shape
    workers = lax.axis_size("yx") * lax.axis_size("core")
    group_index = lax.axis_index("grp")
    core = lax.axis_index("core")
    worker_index = lax.axis_index("yx") * lax.axis_size("core") + core
    grp_orbs = orb_dev * workers
    lanes = 128
    slot_cap = pair_slots.shape[2]
    table = table_lanes(pair_slots, pair_count, box_edge, lanes)[0]
    cores = lax.axis_size("core")
    chips = lax.axis_size("yx")
    swap = [(0, 1), (1, 0)]
    upper_set = passed_along(orbitals, "grp", -1)
    own_part = jnp.concatenate([orbitals[0], table], axis=-1)
    upper_part = jnp.concatenate([upper_set[0], jnp.zeros_like(table)], axis=-1)
    first = core == 0
    keep = jnp.where(first, own_part, upper_part)
    got = lax.ppermute(jnp.where(first, upper_part, own_part), "core", swap)
    chip_pair = jnp.where(first, jnp.stack([keep, got]), jnp.stack([got, keep]))
    sent = jnp.broadcast_to(chip_pair[None], (chips,) + chip_pair.shape)
    collected = lax.all_to_all(sent, "yx", 0, 0, tiled=True).reshape(
        (grp_orbs, box_edge, plane_size + lanes)
    )
    other = lax.ppermute(collected, "core", swap)

    entries = 2 * slot_cap + 1
    digits = jnp.where(
        first,
        collected[:, 0, plane_size : plane_size + 2 * entries],
        other[:, 0, plane_size : plane_size + 2 * entries],
    ).astype(jnp.int32)
    values = digits[:, :entries] * box_edge + digits[:, entries:]
    group_slots = values[:, : 2 * slot_cap].reshape(-1, 2)
    group_count = values[:, 2 * slot_cap]
    per_worker = (slot_cap + 1) // 2
    in_use = (jnp.arange(slot_cap, dtype=jnp.int32)[None, :] < group_count[:, None]).reshape(-1)
    rank = jnp.cumsum(in_use.astype(jnp.int32)) - 1
    wanted = worker_index * per_worker + jnp.arange(per_worker, dtype=jnp.int32)
    match = in_use[None, :] & (rank[None, :] == wanted[:, None])
    pair_list = jnp.sum(jnp.where(match[:, :, None], group_slots[None, :, :], 0), axis=1)
    weights = jnp.any(match, axis=1).astype(jnp.float32)

    base = group_index * grp_orbs
    left_orb = jnp.where(weights > 0, pair_list[:, 0], base)
    right_orb = jnp.where(weights > 0, pair_list[:, 1], base)
    offset_diff = corner_of(right_orb, offsets) - corner_of(left_orb, offsets)
    left_row = jnp.clip(left_orb - base, 0, 2 * grp_orbs - 1)
    right_row = jnp.clip(right_orb - base, 0, 2 * grp_orbs - 1)
    wanted_rows = jnp.concatenate([left_row, right_row])
    in_collected = (wanted_rows < grp_orbs) == first
    slot = wanted_rows % grp_orbs
    both_boxes = jnp.where(
        in_collected[:, None, None],
        jnp.take(collected, slot, axis=0)[:, :, :plane_size],
        jnp.take(other, slot, axis=0)[:, :, :plane_size],
    )
    left_boxes = both_boxes[:per_worker]
    right_boxes = both_boxes[per_worker:]
    row_shift, plane_shift = shift_matrices(offset_diff, box_edge)
    right_field = move_bf16(right_boxes, row_shift, plane_shift)

    sine_rows = sine_table(box_edge)
    plane_sines = plane_table(sine_rows, box_edge)
    symbol = inverse_symbol(box_edge).reshape(box_edge, plane_size)
    left_field = left_boxes.astype(jnp.float32)
    potential = solve_boxes(left_field * right_field, sine_rows, plane_sines, symbol)
    weighted = potential * weights[:, None, None]
    to_left = weighted * right_field
    to_right = unmove_f32(weighted * left_field, row_shift, plane_shift)

    upper = right_row >= grp_orbs
    sent_fields = jnp.where(upper[:, None, None], to_right, 0.0)
    sent_rows = jnp.where(upper, right_row - grp_orbs, 0)
    got_fields = passed_along(sent_fields, "grp", 1)
    got_rows = passed_along(sent_rows, "grp", 1)

    kept_right = jnp.where(upper[:, None, None], 0.0, to_right)
    kept_rows = jnp.where(upper, 0, right_row)
    halves = workers // cores

    def add_into(target, fields, rows, on_core):
        keep = (rows % cores) == on_core
        placed = jnp.where(keep[:, None, None], fields, 0.0)
        return target.at[rows // cores].add(placed)

    fields = jnp.concatenate([to_left, kept_right], axis=0)
    rows = jnp.concatenate([left_row, kept_rows], axis=0)
    empty = jnp.zeros((halves, box_edge, plane_size), jnp.float32)
    theirs = add_into(add_into(empty, fields, rows, cores - 1 - core), got_fields, got_rows, cores - 1 - core)
    mine = add_into(add_into(empty, fields, rows, core), got_fields, got_rows, core)
    received = lax.ppermute(theirs, "core", [(0, 1), (1, 0)])
    half = lax.optimization_barrier(mine) + received
    pieces = lax.all_to_all(half, "yx", 0, 0, tiled=True)
    return jnp.sum(pieces, axis=0, keepdims=True)


def solution(mesh):
    groups, workers = mesh.devices.shape
    split = jax.sharding.Mesh(mesh.devices.reshape(groups, workers // 2, 2), ("grp", "yx", "core"))
    return jax.shard_map(
        local,
        mesh=split,
        in_specs=(
            P(("grp",) + WORKER_AXES, None, None),
            P(),
            P("grp", WORKER_AXES, None, None),
            P("grp", WORKER_AXES),
        ),
        out_specs=P(("grp",) + WORKER_AXES, None, None),
        check_vma=False,
    )
```

```python
import jax
import jax.numpy as jnp
from jax import lax
from jax.sharding import PartitionSpec as P

screen_shift = 0.05
highest = lax.Precision.HIGHEST
WORKER_AXES = ("yx", "core")


def passed_along(value, axis, steps):
    count = lax.axis_size(axis)
    initial, last = (max(0, -steps), min(count, count - steps))
    return lax.ppermute(value, axis, [(source, source + steps) for source in range(initial, last)])


def sine_table(box_edge):
    counting = jnp.arange(box_edge, dtype=jnp.float32) + 1.0
    scaling = jnp.sqrt(2.0 / (box_edge + 1.0))
    return scaling * jnp.sin(jnp.pi * counting[:, None] * counting[None, :] / (box_edge + 1.0))


def inverse_symbol(box_edge):
    counting = jnp.arange(box_edge, dtype=jnp.float32) + 1.0
    eigen_one = 4.0 * jnp.sin(jnp.pi * counting / (2.0 * (box_edge + 1.0))) ** 2
    eigen_sum = eigen_one[:, None, None] + eigen_one[None, :, None] + eigen_one[None, None, :]
    return 1.0 / (eigen_sum + screen_shift)


def shift_matrices(offset_diff, box_edge):
    cell = jnp.arange(box_edge, dtype=jnp.int32)
    row_shift = cell[None, None, :] == (cell[None, :, None] - offset_diff[:, 0, None, None])
    plane = jnp.arange(box_edge * box_edge, dtype=jnp.int32)
    out_y = (plane // box_edge)[None, :, None]
    out_z = (plane % box_edge)[None, :, None]
    in_y = (plane // box_edge)[None, None, :]
    in_z = (plane % box_edge)[None, None, :]
    plane_shift = (in_y == out_y - offset_diff[:, 1, None, None]) & (
        in_z == out_z - offset_diff[:, 2, None, None]
    )
    return row_shift.astype(jnp.float32), plane_shift.astype(jnp.bfloat16)


def move_bf16(boxes, row_shift, plane_shift):
    planes = jnp.einsum("pxc,pyc->pxy", boxes, plane_shift, preferred_element_type=jnp.float32)
    return jnp.einsum("pxa,pac->pxc", row_shift, planes, precision=highest)


def unmove_f32(fields, row_shift, plane_shift):
    rows = jnp.einsum("pax,pac->pxc", row_shift, fields, precision=highest)
    high = lax.reduce_precision(rows, exponent_bits=8, mantissa_bits=7)
    rest = rows - high
    middle = lax.reduce_precision(rest, exponent_bits=8, mantissa_bits=7)
    low = rest - middle
    parts = jnp.concatenate([high, middle, low], axis=1).astype(jnp.bfloat16)
    moved = jnp.einsum("pxc,pcy->pxy", parts, plane_shift, preferred_element_type=jnp.float32)
    box_edge = fields.shape[1]
    return (moved[:, :box_edge] + moved[:, box_edge : 2 * box_edge]) + moved[:, 2 * box_edge :]


def plane_table(sine_rows, box_edge):
    plane = jnp.arange(box_edge * box_edge, dtype=jnp.int32)
    cell = jnp.arange(box_edge, dtype=jnp.int32)

    def spread(pick):
        picked = pick.astype(jnp.float32)
        rows = jnp.dot(picked, sine_rows, precision=highest)
        return jnp.dot(rows, picked.T, precision=highest)

    outer = plane[:, None] // box_edge == cell[None, :]
    inner = plane[:, None] % box_edge == cell[None, :]
    return spread(outer) * spread(inner)


def solve_boxes(density, sine_rows, plane_sines, symbol):
    count_boxes, box_edge, plane_size = density.shape

    def apply_sines(field_block):
        along_first = jnp.einsum("kx,nxf->nkf", sine_rows, field_block, precision=highest)
        flat_rows = along_first.reshape(count_boxes * box_edge, plane_size)
        along_plane = jnp.dot(
            flat_rows, plane_sines, precision=highest, preferred_element_type=jnp.float32
        )
        return along_plane.reshape(count_boxes, box_edge, plane_size)

    spectrum = apply_sines(density) * symbol
    return apply_sines(spectrum)


def corner_of(orbital, offsets):
    listing = jnp.arange(offsets.shape[0], dtype=jnp.int32)
    chosen = orbital[:, None] == listing[None, :]
    return jnp.sum(jnp.where(chosen[:, :, None], offsets[None, :, :], 0), axis=1, dtype=jnp.int32)


def rows_to_orbitals(fields, rows, count):
    chosen = (rows[:, None] == jnp.arange(count, dtype=jnp.int32)[None, :]).astype(jnp.float32)
    flat = fields.reshape(fields.shape[0], -1)
    summed = jnp.einsum("po,pf->of", chosen, flat, precision=highest)
    return summed.reshape((count,) + fields.shape[1:])


def table_lanes(pair_slots, pair_count, box_edge, lanes):
    values = jnp.concatenate([pair_slots[0, 0].reshape(-1), pair_count[0, 0].reshape(1)])
    digits = jnp.concatenate([values // box_edge, values % box_edge]).astype(jnp.bfloat16)
    row = jnp.zeros((lanes,), jnp.bfloat16).at[: digits.shape[0]].set(digits)
    first = (jnp.arange(box_edge, dtype=jnp.int32) == 0)[:, None]
    return jnp.where(first, row[None, :], jnp.zeros((), jnp.bfloat16))[None]


def local(orbitals, offsets, pair_slots, pair_count):
    orb_dev, box_edge, plane_size = orbitals.shape
    workers = lax.axis_size("yx") * lax.axis_size("core")
    group_index = lax.axis_index("grp")
    core = lax.axis_index("core")
    worker_index = lax.axis_index("yx") * lax.axis_size("core") + core
    grp_orbs = orb_dev * workers
    lanes = 128
    slot_cap = pair_slots.shape[2]
    table = table_lanes(pair_slots, pair_count, box_edge, lanes)[0]
    cores = lax.axis_size("core")
    chips = lax.axis_size("yx")
    swap = [(0, 1), (1, 0)]
    upper_set = passed_along(orbitals, "grp", -1)
    own_part = jnp.concatenate([orbitals[0], table], axis=-1)
    upper_part = jnp.concatenate([upper_set[0], jnp.zeros_like(table)], axis=-1)
    first = core == 0
    keep = jnp.where(first, own_part, upper_part)
    got = lax.ppermute(jnp.where(first, upper_part, own_part), "core", swap)
    chip_pair = jnp.where(first, jnp.stack([keep, got]), jnp.stack([got, keep]))
    sine_rows = sine_table(box_edge)
    plane_sines = plane_table(sine_rows, box_edge)
    plane_sines, chip_pair = lax.optimization_barrier((plane_sines, chip_pair))
    sent = jnp.broadcast_to(chip_pair[None], (chips,) + chip_pair.shape)
    collected = lax.all_to_all(sent, "yx", 0, 0, tiled=True).reshape(
        (grp_orbs, box_edge, plane_size + lanes)
    )
    other = lax.ppermute(collected, "core", swap)

    entries = 2 * slot_cap + 1
    digits = jnp.where(
        first,
        collected[:, 0, plane_size : plane_size + 2 * entries],
        other[:, 0, plane_size : plane_size + 2 * entries],
    ).astype(jnp.int32)
    values = digits[:, :entries] * box_edge + digits[:, entries:]
    group_slots = values[:, : 2 * slot_cap].reshape(-1, 2)
    group_count = values[:, 2 * slot_cap]
    per_worker = (slot_cap + 1) // 2
    in_use = (jnp.arange(slot_cap, dtype=jnp.int32)[None, :] < group_count[:, None]).reshape(-1)
    rank = jnp.cumsum(in_use.astype(jnp.int32)) - 1
    wanted = worker_index * per_worker + jnp.arange(per_worker, dtype=jnp.int32)
    match = in_use[None, :] & (rank[None, :] == wanted[:, None])
    pair_list = jnp.sum(jnp.where(match[:, :, None], group_slots[None, :, :], 0), axis=1)
    weights = jnp.any(match, axis=1).astype(jnp.float32)

    base = group_index * grp_orbs
    left_orb = jnp.where(weights > 0, pair_list[:, 0], base)
    right_orb = jnp.where(weights > 0, pair_list[:, 1], base)
    offset_diff = corner_of(right_orb, offsets) - corner_of(left_orb, offsets)
    left_row = jnp.clip(left_orb - base, 0, 2 * grp_orbs - 1)
    right_row = jnp.clip(right_orb - base, 0, 2 * grp_orbs - 1)
    wanted_rows = jnp.concatenate([left_row, right_row])
    in_collected = (wanted_rows < grp_orbs) == first
    slot = wanted_rows % grp_orbs
    both_boxes = jnp.where(
        in_collected[:, None, None],
        jnp.take(collected, slot, axis=0)[:, :, :plane_size],
        jnp.take(other, slot, axis=0)[:, :, :plane_size],
    )
    left_boxes = both_boxes[:per_worker]
    right_boxes = both_boxes[per_worker:]
    row_shift, plane_shift = shift_matrices(offset_diff, box_edge)
    right_field = move_bf16(right_boxes, row_shift, plane_shift)

    symbol = inverse_symbol(box_edge).reshape(box_edge, plane_size)
    left_field = left_boxes.astype(jnp.float32)
    potential = solve_boxes(left_field * right_field, sine_rows, plane_sines, symbol)
    weighted = potential * weights[:, None, None]
    to_left = weighted * right_field
    to_right = unmove_f32(weighted * left_field, row_shift, plane_shift)

    upper = right_row >= grp_orbs
    sent_fields = jnp.where(upper[:, None, None], to_right, 0.0)
    sent_rows = jnp.where(upper, right_row - grp_orbs, 0)
    got_fields = passed_along(sent_fields, "grp", 1)
    got_rows = passed_along(sent_rows, "grp", 1)

    kept_right = jnp.where(upper[:, None, None], 0.0, to_right)
    kept_rows = jnp.where(upper, 0, right_row)
    halves = workers // cores

    def add_into(target, fields, rows, on_core):
        keep = (rows % cores) == on_core
        placed = jnp.where(keep[:, None, None], fields, 0.0)
        return target.at[rows // cores].add(placed)

    fields = jnp.concatenate([to_left, kept_right], axis=0)
    rows = jnp.concatenate([left_row, kept_rows], axis=0)
    empty = jnp.zeros((halves, box_edge, plane_size), jnp.float32)
    theirs = add_into(add_into(empty, fields, rows, cores - 1 - core), got_fields, got_rows, cores - 1 - core)
    mine = add_into(add_into(empty, fields, rows, core), got_fields, got_rows, core)
    received = lax.ppermute(theirs, "core", [(0, 1), (1, 0)])
    half = lax.optimization_barrier(mine) + received
    pieces = lax.all_to_all(half, "yx", 0, 0, tiled=True)
    return jnp.sum(pieces, axis=0, keepdims=True)


def solution(mesh):
    groups, workers = mesh.devices.shape
    split = jax.sharding.Mesh(mesh.devices.reshape(groups, workers // 2, 2), ("grp", "yx", "core"))
    return jax.shard_map(
        local,
        mesh=split,
        in_specs=(
            P(("grp",) + WORKER_AXES, None, None),
            P(),
            P("grp", WORKER_AXES, None, None),
            P("grp", WORKER_AXES),
        ),
        out_specs=P(("grp",) + WORKER_AXES, None, None),
        check_vma=False,
    )
```
